32 devices in a mesh: island: 4 (over z), fsdp: 8 (over y, x, core).
Axes of the slice: x: 2, y: 2, z: 4, core: 2. Of those that a mesh axis runs over, the one named last changes fastest.
Arguments:
- activations: bfloat16 [4, 4096, 8192], P('island', 'fsdp'), may hold values from -150 to 150
- key_cotangents: bfloat16 [4, 4096, 512], P('island', 'fsdp'), may hold values from -60 to 60
- master: float32 [8192, 512], P('fsdp'), may hold values from -6 to 6
- momentum: float32 [8192, 512], P('fsdp'), may hold values from -3 to 3
- island_weights: float32 [4, 8192, 512], P('island', 'fsdp'), may hold values from -6 to 6
- first_moment: float32 [4, 8192, 512], P('island', 'fsdp'), may hold values from -0.0024414062 to 0.0024414062
- second_moment: float32 [4, 8192, 512], P('island', 'fsdp'), may hold values from 5.9604645e-08 to 9.536743e-07
- tile_rows: int32 [48], replicated, may hold values from 1 to 512, 8192 in all
Outputs:
- master_out: float32 [8192, 512], P('fsdp')
- momentum_out: float32 [8192, 512], P('fsdp')
- tile_sums: float32 [48], replicated
The draws below stay inside these ranges and needn't reach their ends.
Inputs may be any that keep to these rules, and one draw needn't show every extreme that they name: `tile_rows`: consecutive tiles covering all 8192 rows; the largest has exactly 512 rows.
All inputs are finite; a program needn't handle non-finite values.
Results may differ from the reference program's by a relative error of at most 0.0003.
Values may be sent and summed in bfloat16 or wider, within the bound.
No kernel may reach another device: no remote copies, remote signals or barrier semaphores. Data moves between devices by JAX's collectives and lax.ppermute only.
A program may use at most 128 MiB of HBM per device.

```python
import math
import jax
import jax.numpy as jnp
import numpy as np
from jax import lax

D = 8192
HEAD = 128
SEQ = 8192
TOK_DEV = 512
TILES = 48
TILE_MOST = 512
KC = 512
ISLANDS = 4
TOK_ISL = 4096


def draw_activations(key, part):
    keys = jax.random.split(key, 3)
    shape = (ISLANDS, TOK_ISL, D)
    values = jnp.clip(jax.random.normal(keys[0], shape, jnp.float32), -5.0, 5.0)
    spread = jnp.log(10.0) * jax.random.uniform(keys[1], (D,), jnp.float32)
    trend = 0.5 * jnp.log(3.0) * jnp.arange(D, dtype=jnp.float32) / D
    scales = jnp.exp(spread + trend)
    blocks = TOK_ISL // TOK_DEV
    order = jax.random.permutation(keys[2], blocks)
    row_block = jnp.arange(TOK_ISL, dtype=jnp.int32) // TOK_DEV
    col_block = jnp.arange(D, dtype=jnp.int32) // (D // blocks)
    boost = jnp.where(order[row_block][:, None] == col_block[None, :], 3.0, 1.0)
    return (0.5 * values * scales[None, None, :] * boost[None, :, :]).astype(jnp.bfloat16)


def draw_key_cotangents(key, part):
    keys = jax.random.split(key, 2)
    shape = (ISLANDS, TOK_ISL, KC)
    values = jnp.clip(jax.random.normal(keys[0], shape, jnp.float32), -5.0, 5.0)
    scales = jnp.exp(jnp.log(10.0) * jax.random.uniform(keys[1], (KC,), jnp.float32))
    return (values * scales[None, None, :]).astype(jnp.bfloat16)


def level_of(key, shape, shards, low, largest):
    def one(dim, blocks):
        heights = jax.random.uniform(jax.random.fold_in(jax.random.fold_in(key, 6), dim), (blocks,), jnp.float32, low / len(shards), largest / len(shards))
        return jnp.repeat(jnp.exp(heights), shape[dim] // blocks).reshape((-1,) + (1,) * (len(shape) - dim - 1))

    factor_of = one(*shards[0])
    for cut in shards[1:]:
        factor_of = factor_of * one(*cut)
    return factor_of


def length_profile(count, total, reach, skew):
    weights = [(1 << 20) // math.isqrt(standing ** skew) + 1 for standing in range(2, count + 1)]
    surplus, given = total - reach - (count - 1), [1] * (count - 1)
    while surplus > 0:
        free = [i for i in range(count - 1) if given[i] < reach]
        pool, left = sum([weights[i] for i in free]), surplus
        for i in free:
            addition = min(reach - given[i], max(1, left * weights[i] // pool), surplus)
            given[i] = given[i] + addition
            surplus = surplus - addition
    return np.array([reach] + given)


def ragged(key, number_of, total, reach, lean):
    if number_of == 2:
        one = jax.random.randint(key, (), max(1, total - reach), min(reach, total - 1) + 1)
        return jnp.stack([one, total - one])
    tallies = jnp.asarray(length_profile(number_of, total, reach, lean), jnp.int32)
    twos = (number_of - 1) // 2
    donor, sink = tallies[1:1 + 2 * twos:2], tallies[2:2 + 2 * twos:2]
    room = jnp.minimum(donor - 1, reach - sink)
    shifted = jax.random.randint(jax.random.fold_in(key, 1), (twos,), 0, 1 << 20) % (room + 1)
    tallies = tallies.at[1:1 + 2 * twos:2].set(donor - shifted).at[2:2 + 2 * twos:2].set(sink + shifted)
    return tallies[jax.random.permutation(jax.random.fold_in(key, 2), number_of)]


def gaussian(rng, extent, deviation, bound, cuts=(), held_as=jnp.bfloat16):
    result = deviation * jax.random.normal(rng, extent, jnp.float32)
    if cuts:
        result = result * level_of(rng, extent, cuts, -0.22, 0.18)
    return jnp.clip(result, -bound, bound).astype(held_as)


def setup_inputs(seed: int = 0) -> dict:
    seeds = jax.random.split(jax.random.key(seed), 9)
    return {
        "activations": draw_activations(jax.random.fold_in(seeds[8], 71), 0),
        "key_cotangents": draw_key_cotangents(jax.random.fold_in(seeds[8], 71), 0),
        "master": gaussian(seeds[2], (D, KC), 1.0, 6.0, ((0, 8),), jnp.float32),
        "momentum": gaussian(seeds[3], (D, KC), 0.5, 3.0, ((0, 8),), jnp.float32),
        "island_weights": gaussian(seeds[4], (ISLANDS, D, KC), 1.0, 6.0, ((0, 4), (1, 8)), jnp.float32),
        "first_moment": gaussian(seeds[5], (ISLANDS, D, KC), ((D * KC) ** -0.5), 0.0024414062, ((0, 4), (1, 8)), jnp.float32),
        "second_moment": jnp.clip(jnp.exp(math.log(9.5367431640625e-07) - 2.7725887 * jax.random.uniform(seeds[6], (ISLANDS, D, KC), jnp.float32) ** level_of(seeds[6], (ISLANDS, D, KC), ((0, 4), (1, 8)), -0.2, 0.2)), 5.960464477539063e-08, 9.5367431640625e-07),
        "tile_rows": ragged(seeds[7], TILES, D, TILE_MOST, 1).astype(jnp.int32),
    }


beta_one = 0.9
beta_two = 0.95
bias_one = 1.0 - 0.9 ** 3
bias_two = 1.0 - 0.95 ** 3
inner_rate = 0.5
decay_rate = 0.1
outer_rate = 0.7
outer_moment = 0.9
adam_eps = 1e-08
norm_epsilon = 1e-06
rope_base = 500000.0

def unrotate(cotangent, first_row):
    rows = cotangent.shape[0]
    half = HEAD // 2
    positions = ((first_row + jnp.arange(rows, dtype=jnp.int32)) % SEQ).astype(jnp.float32)
    rates = rope_base ** (-2.0 * jnp.arange(half).astype(jnp.float32) / HEAD)
    angles = positions[:, None] * rates[None, :]
    cosine = jnp.cos(angles)[:, None, :]
    sine = jnp.sin(angles)[:, None, :]
    heads = cotangent.astype(jnp.float32).reshape(rows, -1, HEAD)
    lower = heads[:, :, :half]
    upper = heads[:, :, half:]
    turned = jnp.concatenate([lower * cosine + upper * sine, upper * cosine - lower * sine], axis=2)
    return turned.reshape(rows, -1).astype(jnp.bfloat16)

def adam_update(gradient, weights, first, second):
    first_new = beta_one * first + (1.0 - beta_one) * gradient
    second_new = beta_two * second + (1.0 - beta_two) * gradient * gradient
    ratio = first_new / bias_one / (jnp.sqrt(second_new / bias_two) + adam_eps)
    return weights - inner_rate * (ratio + decay_rate * weights)

def local_tiles(drift_rows, tile_rows, first_row):
    ends = jnp.cumsum(tile_rows, dtype=jnp.int32)
    starts = ends - tile_rows
    rows = first_row + jnp.arange(drift_rows.shape[0], dtype=jnp.int32)
    member = ((rows[:, None] >= starts[None, :]) & (rows[:, None] < ends[None, :])).astype(jnp.float32)
    return jnp.dot(lax.optimization_barrier(jnp.sum(drift_rows, axis=1)), member, precision=lax.Precision.HIGHEST)

def reference(activations, key_cotangents, master, momentum, island_weights, first_moment, second_moment, tile_rows):
    drift_total = jnp.zeros(master.shape, jnp.float32)
    for island in range(ISLANDS):
        unrotated = unrotate(key_cotangents[island], 0)
        gradient = jnp.dot(activations[island].T, unrotated, preferred_element_type=jnp.float32)
        factor = 1.0 / jnp.sqrt(jnp.sum(gradient * gradient) + norm_epsilon)
        inner = adam_update(gradient * factor, island_weights[island], first_moment[island], second_moment[island])
        drift_total = drift_total + (master - inner)
    drift = drift_total / ISLANDS
    momentum_out = outer_moment * momentum + drift
    master_out = master - outer_rate * (drift + outer_moment * momentum_out)
    totals = local_tiles(drift, tile_rows, 0)
    tile_sums = totals / jnp.sqrt(tile_rows.astype(jnp.float32) * KC)
    return (master_out, momentum_out, tile_sums)
```

```python
import jax
import jax.numpy as jnp
from jax import lax
from jax.sharding import PartitionSpec as P

HEAD = 128
SEQ = 8192


beta_one = 0.9
beta_two = 0.95
bias_one = 1.0 - 0.9**3
bias_two = 1.0 - 0.95**3
inner_rate = 0.5
decay_rate = 0.1
outer_rate = 0.7
outer_moment = 0.9
adam_eps = 1e-08
norm_epsilon = 1e-06
rope_base = 500000.0


def unrotate(cotangent, first_row):
    rows = cotangent.shape[0]
    half = HEAD // 2
    positions = ((first_row + jnp.arange(rows, dtype=jnp.int32)) % SEQ).astype(jnp.float32)
    rates = rope_base ** (-2.0 * jnp.arange(half).astype(jnp.float32) / HEAD)
    angles = positions[:, None] * rates[None, :]
    cosine = jnp.cos(angles)[:, None, :]
    sine = jnp.sin(angles)[:, None, :]
    heads = cotangent.astype(jnp.float32).reshape(rows, -1, HEAD)
    lower = heads[:, :, :half]
    upper = heads[:, :, half:]
    turned = jnp.concatenate([lower * cosine + upper * sine, upper * cosine - lower * sine], axis=2)
    return turned.reshape(rows, -1).astype(jnp.bfloat16)


def adam_update(gradient, weights, first, second):
    first_new = beta_one * first + (1.0 - beta_one) * gradient
    second_new = beta_two * second + (1.0 - beta_two) * gradient * gradient
    ratio = first_new / bias_one / (jnp.sqrt(second_new / bias_two) + adam_eps)
    return weights - inner_rate * (ratio + decay_rate * weights)


def local_tiles(drift_rows, tile_rows, first_row):
    ends = jnp.cumsum(tile_rows, dtype=jnp.int32)
    starts = ends - tile_rows
    rows = first_row + jnp.arange(drift_rows.shape[0], dtype=jnp.int32)
    member = ((rows[:, None] >= starts[None, :]) & (rows[:, None] < ends[None, :])).astype(
        jnp.float32
    )
    return jnp.dot(jnp.sum(drift_rows, axis=1), member, precision=lax.Precision.HIGHEST)


def body(
    activations,
    key_cotangents,
    master,
    momentum,
    island_weights,
    first_moment,
    second_moment,
    tile_rows,
):
    own_rows = master.shape[0]
    position = lax.axis_index("fsdp")
    columns = lax.all_to_all(activations[0], "fsdp", 1, 0, tiled=True)
    tok_rows = key_cotangents.shape[1]
    unrotated = lax.all_gather(
        unrotate(key_cotangents[0], position * tok_rows), "fsdp", axis=0, tiled=True
    )
    gradient = lax.dot_general(
        columns, unrotated, (((0,), (0,)), ((), ())), preferred_element_type=jnp.float32
    )
    squares = lax.psum(jnp.sum(gradient * gradient), "fsdp")
    factor = 1.0 / jnp.sqrt(squares + norm_epsilon)
    inner = adam_update(gradient * factor, island_weights[0], first_moment[0], second_moment[0])
    island_drift = master - inner
    replicas = lax.axis_size("island")
    drift = lax.psum(island_drift, "island") / replicas
    momentum_out = outer_moment * momentum + drift
    master_out = master - outer_rate * (drift + outer_moment * momentum_out)
    first_row = position * own_rows
    totals = lax.psum(local_tiles(drift, tile_rows, first_row), "fsdp")
    tile_sums = totals / jnp.sqrt(tile_rows.astype(jnp.float32) * master.shape[1])
    return (master_out, momentum_out, tile_sums)


def solution(mesh):
    placed = (
        P("island", "fsdp", None),
        P("island", "fsdp", None),
        P("fsdp", None),
        P("fsdp", None),
        P("island", "fsdp", None),
        P("island", "fsdp", None),
        P("island", "fsdp", None),
        P(),
    )
    return jax.shard_map(
        body,
        mesh=mesh,
        in_specs=placed,
        out_specs=(P("fsdp", None), P("fsdp", None), P()),
        check_vma=False,
    )
```

```python
import jax
import jax.numpy as jnp
from jax import lax
from jax.sharding import PartitionSpec as P

HEAD = 128
SEQ = 8192


beta_one = 0.9
beta_two = 0.95
bias_one = 1.0 - 0.9**3
bias_two = 1.0 - 0.95**3
inner_rate = 0.5
decay_rate = 0.1
outer_rate = 0.7
outer_moment = 0.9
adam_eps = 1e-08
norm_epsilon = 1e-06
rope_base = 500000.0


def unrotate(cotangent, first_row):
    rows = cotangent.shape[0]
    half = HEAD // 2
    positions = ((first_row + jnp.arange(rows, dtype=jnp.int32)) % SEQ).astype(jnp.float32)
    rates = rope_base ** (-2.0 * jnp.arange(half).astype(jnp.float32) / HEAD)
    angles = positions[:, None] * rates[None, :]
    cosine = jnp.cos(angles)[:, None, :]
    sine = jnp.sin(angles)[:, None, :]
    heads = cotangent.astype(jnp.float32).reshape(rows, -1, HEAD)
    lower = heads[:, :, :half]
    upper = heads[:, :, half:]
    turned = jnp.concatenate([lower * cosine + upper * sine, upper * cosine - lower * sine], axis=2)
    return turned.reshape(rows, -1).astype(jnp.bfloat16)


def adam_update(gradient, weights, first, second):
    first_new = beta_one * first + (1.0 - beta_one) * gradient
    second_new = beta_two * second + (1.0 - beta_two) * gradient * gradient
    ratio = first_new / bias_one / (jnp.sqrt(second_new / bias_two) + adam_eps)
    return weights - inner_rate * (ratio + decay_rate * weights)


def local_tiles(drift_rows, tile_rows, first_row):
    ends = jnp.cumsum(tile_rows, dtype=jnp.int32)
    starts = ends - tile_rows
    rows = first_row + jnp.arange(drift_rows.shape[0], dtype=jnp.int32)
    member = ((rows[:, None] >= starts[None, :]) & (rows[:, None] < ends[None, :])).astype(
        jnp.float32
    )
    return jnp.dot(jnp.sum(drift_rows, axis=1), member, precision=lax.Precision.HIGHEST)


def body(
    activations,
    key_cotangents,
    master,
    momentum,
    island_weights,
    first_moment,
    second_moment,
    tile_rows,
):
    own_rows = master.shape[0]
    tok_rows = key_cotangents.shape[1]
    chips = lax.axis_size("chip")
    core = lax.axis_index("core")
    position = lax.axis_index("chip") * 2 + core
    swap = [(0, 1), (1, 0)]
    unrotated = unrotate(key_cotangents[0], position * tok_rows)
    blocks = activations[0].reshape(tok_rows, chips, 2, own_rows)
    mine = lax.dynamic_index_in_dim(blocks, core, axis=2, keepdims=False)
    other = lax.dynamic_index_in_dim(blocks, 1 - core, axis=2, keepdims=False)
    their_tokens = lax.ppermute(other, "core", swap)
    their_unrotated = lax.ppermute(unrotated, "core", swap)
    contract = (((0,), (0,)), ((), ()))
    partial = lax.dot_general(
        mine.reshape(tok_rows, chips * own_rows), unrotated, contract,
        preferred_element_type=jnp.float32,
    ) + lax.dot_general(
        their_tokens.reshape(tok_rows, chips * own_rows), their_unrotated, contract,
        preferred_element_type=jnp.float32,
    )
    gradient = lax.psum_scatter(partial, "chip", scatter_dimension=0, tiled=True)
    squares = lax.psum(jnp.sum(gradient * gradient), ("chip", "core"))
    factor = 1.0 / jnp.sqrt(squares + norm_epsilon)
    inner = adam_update(gradient * factor, island_weights[0], first_moment[0], second_moment[0])
    island_drift = master - inner
    replicas = lax.axis_size("island")
    drift = lax.psum(island_drift, "island") / replicas
    momentum_out = outer_moment * momentum + drift
    master_out = master - outer_rate * (drift + outer_moment * momentum_out)
    first_row = position * own_rows
    totals = (
        lax.psum(local_tiles(island_drift, tile_rows, first_row), ("island", "chip", "core"))
        / replicas
    )
    tile_sums = totals / jnp.sqrt(tile_rows.astype(jnp.float32) * master.shape[1])
    return (master_out, momentum_out, tile_sums)


def solution(mesh):
    islands, fsdp = mesh.devices.shape
    cores = jax.sharding.Mesh(
        mesh.devices.reshape(islands, fsdp // 2, 2), ("island", "chip", "core")
    )
    rows = ("chip", "core")
    placed = (
        P("island", rows, None),
        P("island", rows, None),
        P(rows, None),
        P(rows, None),
        P("island", rows, None),
        P("island", rows, None),
        P("island", rows, None),
        P(),
    )
    return jax.shard_map(
        body,
        mesh=cores,
        in_specs=placed,
        out_specs=(P(rows, None), P(rows, None), P()),
        check_vma=False,
    )
```

```python
import jax
import jax.numpy as jnp
from jax import lax
from jax.sharding import PartitionSpec as P

HEAD = 128
SEQ = 8192


beta_one = 0.9
beta_two = 0.95
bias_one = 1.0 - 0.9**3
bias_two = 1.0 - 0.95**3
inner_rate = 0.5
decay_rate = 0.1
outer_rate = 0.7
outer_moment = 0.9
adam_eps = 1e-08
norm_epsilon = 1e-06
rope_base = 500000.0


def unrotate(cotangent, first_row):
    rows = cotangent.shape[0]
    half = HEAD // 2
    positions = ((first_row + jnp.arange(rows, dtype=jnp.int32)) % SEQ).astype(jnp.float32)
    rates = rope_base ** (-2.0 * jnp.arange(half).astype(jnp.float32) / HEAD)
    angles = positions[:, None] * rates[None, :]
    cosine = jnp.cos(angles)[:, None, :]
    sine = jnp.sin(angles)[:, None, :]
    heads = cotangent.astype(jnp.float32).reshape(rows, -1, HEAD)
    lower = heads[:, :, :half]
    upper = heads[:, :, half:]
    turned = jnp.concatenate([lower * cosine + upper * sine, upper * cosine - lower * sine], axis=2)
    return turned.reshape(rows, -1).astype(jnp.bfloat16)


def adam_update(gradient, weights, first, second):
    first_new = beta_one * first + (1.0 - beta_one) * gradient
    second_new = beta_two * second + (1.0 - beta_two) * gradient * gradient
    ratio = first_new / bias_one / (jnp.sqrt(second_new / bias_two) + adam_eps)
    return weights - inner_rate * (ratio + decay_rate * weights)


def local_tiles(drift_rows, tile_rows, first_row):
    ends = jnp.cumsum(tile_rows, dtype=jnp.int32)
    starts = ends - tile_rows
    rows = first_row + jnp.arange(drift_rows.shape[0], dtype=jnp.int32)
    member = ((rows[:, None] >= starts[None, :]) & (rows[:, None] < ends[None, :])).astype(
        jnp.float32
    )
    return jnp.dot(jnp.sum(drift_rows, axis=1), member, precision=lax.Precision.HIGHEST)


def body(
    activations,
    key_cotangents,
    master,
    momentum,
    island_weights,
    first_moment,
    second_moment,
    tile_rows,
):
    own_rows = master.shape[0]
    tok_rows = key_cotangents.shape[1]
    chips = lax.axis_size("chip")
    core = lax.axis_index("core")
    position = lax.axis_index("chip") * 2 + core
    swap = [(0, 1), (1, 0)]
    unrotated = unrotate(key_cotangents[0], position * tok_rows)
    tokens = activations[0]

    def parity(side):
        return jnp.stack(
            [
                lax.dynamic_slice_in_dim(tokens, (2 * k + side) * own_rows, own_rows, axis=1)
                for k in range(chips)
            ],
            axis=1,
        )

    their_tokens = lax.ppermute(parity(1 - core), "core", swap)
    their_unrotated = lax.ppermute(unrotated, "core", swap)
    contract = (((0,), (0,)), ((), ()))
    partial = lax.dot_general(
        unrotated, parity(core), contract, preferred_element_type=jnp.float32
    ) + lax.dot_general(
        their_unrotated, their_tokens, contract, preferred_element_type=jnp.float32
    )
    gradient = lax.psum_scatter(partial, "chip", scatter_dimension=1, tiled=True)
    gradient = gradient.reshape(gradient.shape[0], own_rows).T
    squares = lax.psum(jnp.sum(gradient * gradient), ("chip", "core"))
    factor = 1.0 / jnp.sqrt(squares + norm_epsilon)
    inner = adam_update(gradient * factor, island_weights[0], first_moment[0], second_moment[0])
    island_drift = master - inner
    replicas = lax.axis_size("island")
    drift = lax.psum(island_drift, "island") / replicas
    momentum_out = outer_moment * momentum + drift
    master_out = master - outer_rate * (drift + outer_moment * momentum_out)
    first_row = position * own_rows
    totals = (
        lax.psum(local_tiles(island_drift, tile_rows, first_row), ("island", "chip", "core"))
        / replicas
    )
    tile_sums = totals / jnp.sqrt(tile_rows.astype(jnp.float32) * master.shape[1])
    return (master_out, momentum_out, tile_sums)


def solution(mesh):
    islands, fsdp = mesh.devices.shape
    cores = jax.sharding.Mesh(
        mesh.devices.reshape(islands, fsdp // 2, 2), ("island", "chip", "core")
    )
    rows = ("chip", "core")
    placed = (
        P("island", rows, None),
        P("island", rows, None),
        P(rows, None),
        P(rows, None),
        P("island", rows, None),
        P("island", rows, None),
        P("island", rows, None),
        P(),
    )
    return jax.shard_map(
        body,
        mesh=cores,
        in_specs=placed,
        out_specs=(P(rows, None), P(rows, None), P()),
        check_vma=False,
    )
```

```python
import jax
import jax.numpy as jnp
from jax import lax
from jax.experimental.layout import Layout, with_layout_constraint
from jax.sharding import PartitionSpec as P

HEAD = 128
SEQ = 8192


beta_one = 0.9
beta_two = 0.95
bias_one = 1.0 - 0.9**3
bias_two = 1.0 - 0.95**3
inner_rate = 0.5
decay_rate = 0.1
outer_rate = 0.7
outer_moment = 0.9
adam_eps = 1e-08
norm_epsilon = 1e-06
rope_base = 500000.0


def unrotate(cotangent, first_row):
    rows = cotangent.shape[0]
    half = HEAD // 2
    positions = ((first_row + jnp.arange(rows, dtype=jnp.int32)) % SEQ).astype(jnp.float32)
    rates = rope_base ** (-2.0 * jnp.arange(half).astype(jnp.float32) / HEAD)
    angles = positions[:, None] * rates[None, :]
    cosine = jnp.cos(angles)[:, None, :]
    sine = jnp.sin(angles)[:, None, :]
    heads = cotangent.astype(jnp.float32).reshape(rows, -1, HEAD)
    lower = heads[:, :, :half]
    upper = heads[:, :, half:]
    turned = jnp.concatenate([lower * cosine + upper * sine, upper * cosine - lower * sine], axis=2)
    return turned.reshape(rows, -1).astype(jnp.bfloat16)


def adam_update(gradient, weights, first, second):
    first_new = beta_one * first + (1.0 - beta_one) * gradient
    second_new = beta_two * second + (1.0 - beta_two) * gradient * gradient
    ratio = first_new / bias_one / (jnp.sqrt(second_new / bias_two) + adam_eps)
    return weights - inner_rate * (ratio + decay_rate * weights)


def local_tiles(drift_rows, tile_rows, first_row):
    ends = jnp.cumsum(tile_rows, dtype=jnp.int32)
    starts = ends - tile_rows
    rows = first_row + jnp.arange(drift_rows.shape[0], dtype=jnp.int32)
    member = ((rows[:, None] >= starts[None, :]) & (rows[:, None] < ends[None, :])).astype(
        jnp.float32
    )
    return jnp.dot(jnp.sum(drift_rows, axis=1), member, precision=lax.Precision.HIGHEST)


def body(
    activations,
    key_cotangents,
    master,
    momentum,
    island_weights,
    first_moment,
    second_moment,
    tile_rows,
):
    own_rows = master.shape[0]
    tok_rows = key_cotangents.shape[1]
    chips = lax.axis_size("chip")
    core = lax.axis_index("core")
    position = lax.axis_index("chip") * 2 + core
    swap = [(0, 1), (1, 0)]
    unrotated = unrotate(key_cotangents[0], position * tok_rows)
    tokens = activations[0]

    def parity(side):
        return jnp.stack(
            [
                lax.dynamic_slice_in_dim(tokens, (2 * k + side) * own_rows, own_rows, axis=1)
                for k in range(chips)
            ],
            axis=1,
        )

    their_tokens = lax.ppermute(parity(1 - core), "core", swap)
    their_unrotated = lax.ppermute(unrotated, "core", swap)
    contract = (((0,), (0,)), ((), ()))
    partial = lax.dot_general(
        unrotated, parity(core), contract, preferred_element_type=jnp.float32
    ) + lax.dot_general(
        their_unrotated, their_tokens, contract, preferred_element_type=jnp.float32
    )
    partial = with_layout_constraint(partial, Layout((1, 2, 0)))
    gradient = lax.psum_scatter(partial, "chip", scatter_dimension=1, tiled=True)
    gradient = with_layout_constraint(
        gradient.reshape(gradient.shape[0], own_rows).T, Layout((0, 1))
    )
    squares = lax.psum(jnp.sum(gradient * gradient), ("chip", "core"))
    factor = 1.0 / jnp.sqrt(squares + norm_epsilon)
    inner = adam_update(gradient * factor, island_weights[0], first_moment[0], second_moment[0])
    island_drift = master - inner
    replicas = lax.axis_size("island")
    drift = lax.psum(island_drift, "island") / replicas
    momentum_out = outer_moment * momentum + drift
    master_out = master - outer_rate * (drift + outer_moment * momentum_out)
    first_row = position * own_rows
    totals = (
        lax.psum(local_tiles(island_drift, tile_rows, first_row), ("island", "chip", "core"))
        / replicas
    )
    tile_sums = totals / jnp.sqrt(tile_rows.astype(jnp.float32) * master.shape[1])
    return (master_out, momentum_out, tile_sums)


def solution(mesh):
    islands, fsdp = mesh.devices.shape
    cores = jax.sharding.Mesh(
        mesh.devices.reshape(islands, fsdp // 2, 2), ("island", "chip", "core")
    )
    rows = ("chip", "core")
    placed = (
        P("island", rows, None),
        P("island", rows, None),
        P(rows, None),
        P(rows, None),
        P("island", rows, None),
        P("island", rows, None),
        P("island", rows, None),
        P(),
    )
    return jax.shard_map(
        body,
        mesh=cores,
        in_specs=placed,
        out_specs=(P(rows, None), P(rows, None), P()),
        check_vma=False,
    )
```

```python
import jax
import jax.numpy as jnp
from jax import lax
from jax.experimental.layout import Layout, with_layout_constraint
from jax.sharding import PartitionSpec as P

HEAD = 128
SEQ = 8192


beta_one = 0.9
beta_two = 0.95
bias_one = 1.0 - 0.9**3
bias_two = 1.0 - 0.95**3
inner_rate = 0.5
decay_rate = 0.1
outer_rate = 0.7
outer_moment = 0.9
adam_eps = 1e-08
norm_epsilon = 1e-06
rope_base = 500000.0


def unrotate(cotangent, first_row):
    rows = cotangent.shape[0]
    half = HEAD // 2
    positions = ((first_row + jnp.arange(rows, dtype=jnp.int32)) % SEQ).astype(jnp.float32)
    rates = rope_base ** (-2.0 * jnp.arange(half).astype(jnp.float32) / HEAD)
    angles = positions[:, None] * rates[None, :]
    cosine = jnp.cos(angles)[:, None, :]
    sine = jnp.sin(angles)[:, None, :]
    heads = cotangent.astype(jnp.float32).reshape(rows, -1, HEAD)
    lower = heads[:, :, :half]
    upper = heads[:, :, half:]
    turned = jnp.concatenate([lower * cosine + upper * sine, upper * cosine - lower * sine], axis=2)
    return turned.reshape(rows, -1).astype(jnp.bfloat16)


def adam_update(gradient, weights, first, second):
    first_new = beta_one * first + (1.0 - beta_one) * gradient
    second_new = beta_two * second + (1.0 - beta_two) * gradient * gradient
    ratio = first_new / bias_one / (jnp.sqrt(second_new / bias_two) + adam_eps)
    return weights - inner_rate * (ratio + decay_rate * weights)


def local_tiles(drift_rows, tile_rows, first_row):
    ends = jnp.cumsum(tile_rows, dtype=jnp.int32)
    starts = ends - tile_rows
    rows = first_row + jnp.arange(drift_rows.shape[0], dtype=jnp.int32)
    member = ((rows[:, None] >= starts[None, :]) & (rows[:, None] < ends[None, :])).astype(
        jnp.float32
    )
    return jnp.dot(jnp.sum(drift_rows, axis=1), member, precision=lax.Precision.HIGHEST)


def body(
    activations,
    key_cotangents,
    master,
    momentum,
    island_weights,
    first_moment,
    second_moment,
    tile_rows,
):
    own_rows = master.shape[0]
    tok_rows = key_cotangents.shape[1]
    chips = lax.axis_size("chip")
    core = lax.axis_index("core")
    position = lax.axis_index("chip") * 2 + core
    swap = [(0, 1), (1, 0)]
    unrotated = unrotate(key_cotangents[0], position * tok_rows)
    tokens = activations[0]

    def parity(side):
        return jnp.stack(
            [
                lax.dynamic_slice_in_dim(tokens, (2 * k + side) * own_rows, own_rows, axis=1)
                for k in range(chips)
            ],
            axis=1,
        )

    their_tokens = lax.ppermute(parity(1 - core), "core", swap)
    their_unrotated = lax.ppermute(unrotated, "core", swap)
    contract = (((0,), (0,)), ((), ()))
    partial = lax.dot_general(
        unrotated, parity(core), contract, preferred_element_type=jnp.float32
    ) + lax.dot_general(
        their_unrotated, their_tokens, contract, preferred_element_type=jnp.float32
    )
    gradient = lax.psum_scatter(partial, "chip", scatter_dimension=1, tiled=True)
    gradient = with_layout_constraint(gradient, Layout((0, 1, 2)))
    gradient = with_layout_constraint(
        gradient.reshape(gradient.shape[0], own_rows).T, Layout((0, 1))
    )
    squares = lax.psum(jnp.sum(gradient * gradient), ("chip", "core"))
    factor = 1.0 / jnp.sqrt(squares + norm_epsilon)
    inner = adam_update(gradient * factor, island_weights[0], first_moment[0], second_moment[0])
    island_drift = master - inner
    replicas = lax.axis_size("island")
    drift = lax.psum(island_drift, "island") / replicas
    momentum_out = outer_moment * momentum + drift
    master_out = master - outer_rate * (drift + outer_moment * momentum_out)
    first_row = position * own_rows
    totals = (
        lax.psum(local_tiles(island_drift, tile_rows, first_row), ("island", "chip", "core"))
        / replicas
    )
    tile_sums = totals / jnp.sqrt(tile_rows.astype(jnp.float32) * master.shape[1])
    return (master_out, momentum_out, tile_sums)


def solution(mesh):
    islands, fsdp = mesh.devices.shape
    cores = jax.sharding.Mesh(
        mesh.devices.reshape(islands, fsdp // 2, 2), ("island", "chip", "core")
    )
    rows = ("chip", "core")
    placed = (
        P("island", rows, None),
        P("island", rows, None),
        P(rows, None),
        P(rows, None),
        P("island", rows, None),
        P("island", rows, None),
        P("island", rows, None),
        P(),
    )
    return jax.shard_map(
        body,
        mesh=cores,
        in_specs=placed,
        out_specs=(P(rows, None), P(rows, None), P()),
        check_vma=False,
    )
```

```python
import jax
import jax.numpy as jnp
from jax import lax
from jax.experimental.layout import Layout, with_layout_constraint
from jax.sharding import PartitionSpec as P

HEAD = 128
SEQ = 8192


beta_one = 0.9
beta_two = 0.95
bias_one = 1.0 - 0.9**3
bias_two = 1.0 - 0.95**3
inner_rate = 0.5
decay_rate = 0.1
outer_rate = 0.7
outer_moment = 0.9
adam_eps = 1e-08
norm_epsilon = 1e-06
rope_base = 500000.0


def unrotate(cotangent, first_row):
    rows = cotangent.shape[0]
    half = HEAD // 2
    positions = ((first_row + jnp.arange(rows, dtype=jnp.int32)) % SEQ).astype(jnp.float32)
    rates = rope_base ** (-2.0 * jnp.arange(half).astype(jnp.float32) / HEAD)
    angles = positions[:, None] * rates[None, :]
    cosine = jnp.cos(angles)[:, None, :]
    sine = jnp.sin(angles)[:, None, :]
    heads = cotangent.astype(jnp.float32).reshape(rows, -1, HEAD)
    lower = heads[:, :, :half]
    upper = heads[:, :, half:]
    turned = jnp.concatenate([lower * cosine + upper * sine, upper * cosine - lower * sine], axis=2)
    return turned.reshape(rows, -1).astype(jnp.bfloat16)


def adam_update(gradient, weights, first, second):
    first_new = beta_one * first + (1.0 - beta_one) * gradient
    second_new = beta_two * second + (1.0 - beta_two) * gradient * gradient
    ratio = first_new / bias_one / (jnp.sqrt(second_new / bias_two) + adam_eps)
    return weights - inner_rate * (ratio + decay_rate * weights)


def local_tiles(drift_rows, tile_rows, first_row):
    ends = jnp.cumsum(tile_rows, dtype=jnp.int32)
    starts = ends - tile_rows
    rows = first_row + jnp.arange(drift_rows.shape[0], dtype=jnp.int32)
    member = ((rows[:, None] >= starts[None, :]) & (rows[:, None] < ends[None, :])).astype(
        jnp.float32
    )
    return jnp.dot(jnp.sum(drift_rows, axis=1), member, precision=lax.Precision.HIGHEST)


def body(
    activations,
    key_cotangents,
    master,
    momentum,
    island_weights,
    first_moment,
    second_moment,
    tile_rows,
):
    own_rows = master.shape[0]
    tok_rows = key_cotangents.shape[1]
    chips = lax.axis_size("chip")
    core = lax.axis_index("core")
    position = lax.axis_index("chip") * 2 + core
    swap = [(0, 1), (1, 0)]
    unrotated = unrotate(key_cotangents[0], position * tok_rows)
    tokens = activations[0]

    def parity(side):
        return jnp.stack(
            [
                lax.dynamic_slice_in_dim(tokens, (2 * k + side) * own_rows, own_rows, axis=1)
                for k in range(chips)
            ],
            axis=1,
        )

    their_tokens = lax.ppermute(parity(1 - core), "core", swap)
    their_unrotated = lax.ppermute(unrotated, "core", swap)
    contract = (((0,), (0,)), ((), ()))
    partial = lax.dot_general(
        unrotated, parity(core), contract, preferred_element_type=jnp.float32
    ) + lax.dot_general(
        their_unrotated, their_tokens, contract, preferred_element_type=jnp.float32
    )
    gradient = lax.psum_scatter(partial, "chip", scatter_dimension=1, tiled=True)
    gradient = with_layout_constraint(gradient, Layout((0, 1, 2)))
    gradient = with_layout_constraint(
        gradient.reshape(gradient.shape[0], own_rows).T, Layout((0, 1))
    )
    squares = lax.psum(lax.psum(jnp.sum(gradient * gradient), "core"), "chip")
    factor = 1.0 / jnp.sqrt(squares + norm_epsilon)
    inner = adam_update(gradient * factor, island_weights[0], first_moment[0], second_moment[0])
    island_drift = master - inner
    replicas = lax.axis_size("island")
    drift = lax.psum(island_drift, "island") / replicas
    momentum_out = outer_moment * momentum + drift
    master_out = master - outer_rate * (drift + outer_moment * momentum_out)
    first_row = position * own_rows
    totals = (
        lax.psum(local_tiles(island_drift, tile_rows, first_row), ("island", "chip", "core"))
        / replicas
    )
    tile_sums = totals / jnp.sqrt(tile_rows.astype(jnp.float32) * master.shape[1])
    return (master_out, momentum_out, tile_sums)


def solution(mesh):
    islands, fsdp = mesh.devices.shape
    cores = jax.sharding.Mesh(
        mesh.devices.reshape(islands, fsdp // 2, 2), ("island", "chip", "core")
    )
    rows = ("chip", "core")
    placed = (
        P("island", rows, None),
        P("island", rows, None),
        P(rows, None),
        P(rows, None),
        P("island", rows, None),
        P("island", rows, None),
        P("island", rows, None),
        P(),
    )
    return jax.shard_map(
        body,
        mesh=cores,
        in_specs=placed,
        out_specs=(P(rows, None), P(rows, None), P()),
        check_vma=False,
    )
```

```python
import jax
import jax.numpy as jnp
from jax import lax
from jax.experimental.layout import Layout, with_layout_constraint
from jax.sharding import PartitionSpec as P

HEAD = 128
SEQ = 8192


beta_one = 0.9
beta_two = 0.95
bias_one = 1.0 - 0.9**3
bias_two = 1.0 - 0.95**3
inner_rate = 0.5
decay_rate = 0.1
outer_rate = 0.7
outer_moment = 0.9
adam_eps = 1e-08
norm_epsilon = 1e-06
rope_base = 500000.0


def unrotate(cotangent, first_row):
    rows = cotangent.shape[0]
    half = HEAD // 2
    positions = ((first_row + jnp.arange(rows, dtype=jnp.int32)) % SEQ).astype(jnp.float32)
    rates = rope_base ** (-2.0 * jnp.arange(half).astype(jnp.float32) / HEAD)
    angles = positions[:, None] * rates[None, :]
    cosine = jnp.cos(angles)[:, None, :]
    sine = jnp.sin(angles)[:, None, :]
    heads = cotangent.astype(jnp.float32).reshape(rows, -1, HEAD)
    lower = heads[:, :, :half]
    upper = heads[:, :, half:]
    turned = jnp.concatenate([lower * cosine + upper * sine, upper * cosine - lower * sine], axis=2)
    return turned.reshape(rows, -1).astype(jnp.bfloat16)


def adam_update(gradient, weights, first, second):
    first_new = beta_one * first + (1.0 - beta_one) * gradient
    second_new = beta_two * second + (1.0 - beta_two) * gradient * gradient
    ratio = first_new / bias_one / (jnp.sqrt(second_new / bias_two) + adam_eps)
    return weights - inner_rate * (ratio + decay_rate * weights)


def local_tiles(drift_rows, tile_rows, first_row):
    ends = jnp.cumsum(tile_rows, dtype=jnp.int32)
    starts = ends - tile_rows
    rows = first_row + jnp.arange(drift_rows.shape[0], dtype=jnp.int32)
    member = ((rows[:, None] >= starts[None, :]) & (rows[:, None] < ends[None, :])).astype(
        jnp.float32
    )
    return jnp.dot(jnp.sum(drift_rows, axis=1), member, precision=lax.Precision.HIGHEST)


def island_sum(values, replicas, pieces=4):
    if replicas != 4:
        return lax.psum(values, "island")
    island = lax.axis_index("island")
    middle = (island == 1) | (island == 2)
    rows = values.shape[0] // pieces
    sums, arrived = [], None
    for piece in range(pieces):
        part = values[piece * rows : (piece + 1) * rows]
        if arrived is not None:
            part, _ = lax.optimization_barrier((part, arrived))
        arrived = lax.ppermute(part, "island", [(0, 1), (3, 2)])
        pair = part + arrived
        whole = pair + lax.ppermute(pair, "island", [(1, 2), (2, 1)])
        back = lax.ppermute(whole, "island", [(1, 0), (2, 3)])
        sums.append(jnp.where(middle, whole, back))
    return jnp.concatenate(sums, axis=0)


def body(
    activations,
    key_cotangents,
    master,
    momentum,
    island_weights,
    first_moment,
    second_moment,
    tile_rows,
):
    own_rows = master.shape[0]
    tok_rows = key_cotangents.shape[1]
    chips = lax.axis_size("chip")
    core = lax.axis_index("core")
    position = lax.axis_index("chip") * 2 + core
    swap = [(0, 1), (1, 0)]
    unrotated = unrotate(key_cotangents[0], position * tok_rows)
    tokens = activations[0]

    def parity(side):
        return jnp.stack(
            [
                lax.dynamic_slice_in_dim(tokens, (2 * k + side) * own_rows, own_rows, axis=1)
                for k in range(chips)
            ],
            axis=1,
        )

    their_tokens = lax.ppermute(parity(1 - core), "core", swap)
    their_unrotated = lax.ppermute(unrotated, "core", swap)
    contract = (((0,), (0,)), ((), ()))
    partial = lax.dot_general(
        unrotated, parity(core), contract, preferred_element_type=jnp.float32
    ) + lax.dot_general(
        their_unrotated, their_tokens, contract, preferred_element_type=jnp.float32
    )
    gradient = lax.psum_scatter(partial, "chip", scatter_dimension=1, tiled=True)
    gradient = with_layout_constraint(gradient, Layout((0, 1, 2)))
    gradient = with_layout_constraint(
        gradient.reshape(gradient.shape[0], own_rows).T, Layout((0, 1))
    )
    squares = lax.psum(jnp.sum(gradient * gradient), ("chip", "core"))
    factor = 1.0 / jnp.sqrt(squares + norm_epsilon)
    inner = adam_update(gradient * factor, island_weights[0], first_moment[0], second_moment[0])
    island_drift = master - inner
    replicas = lax.axis_size("island")
    first_row = position * own_rows
    everyone = ("island", "chip", "core")
    partials = local_tiles(island_drift, tile_rows, first_row)
    padded = jnp.zeros((65536,), jnp.float32).at[: partials.shape[0]].set(partials)
    totals = lax.psum(padded, everyone)[: partials.shape[0]] / replicas
    drift = island_sum(island_drift, replicas) / replicas
    momentum_out = outer_moment * momentum + drift
    master_out = master - outer_rate * (drift + outer_moment * momentum_out)
    tile_sums = totals / jnp.sqrt(tile_rows.astype(jnp.float32) * master.shape[1])
    return (master_out, momentum_out, tile_sums)


def solution(mesh):
    islands, fsdp = mesh.devices.shape
    cores = jax.sharding.Mesh(
        mesh.devices.reshape(islands, fsdp // 2, 2), ("island", "chip", "core")
    )
    rows = ("chip", "core")
    placed = (
        P("island", rows, None),
        P("island", rows, None),
        P(rows, None),
        P(rows, None),
        P("island", rows, None),
        P("island", rows, None),
        P("island", rows, None),
        P(),
    )
    return jax.shard_map(
        body,
        mesh=cores,
        in_specs=placed,
        out_specs=(P(rows, None), P(rows, None), P()),
        check_vma=False,
    )
```

```python
import jax
import jax.numpy as jnp
from jax import lax
from jax.experimental.layout import Layout, with_layout_constraint
from jax.sharding import PartitionSpec as P

HEAD = 128
SEQ = 8192


beta_one = 0.9
beta_two = 0.95
bias_one = 1.0 - 0.9**3
bias_two = 1.0 - 0.95**3
inner_rate = 0.5
decay_rate = 0.1
outer_rate = 0.7
outer_moment = 0.9
adam_eps = 1e-08
norm_epsilon = 1e-06
rope_base = 500000.0


def unrotate(cotangent, first_row):
    rows = cotangent.shape[0]
    half = HEAD // 2
    positions = ((first_row + jnp.arange(rows, dtype=jnp.int32)) % SEQ).astype(jnp.float32)
    rates = rope_base ** (-2.0 * jnp.arange(half).astype(jnp.float32) / HEAD)
    angles = positions[:, None] * rates[None, :]
    cosine = jnp.cos(angles)[:, None, :]
    sine = jnp.sin(angles)[:, None, :]
    heads = cotangent.astype(jnp.float32).reshape(rows, -1, HEAD)
    lower = heads[:, :, :half]
    upper = heads[:, :, half:]
    turned = jnp.concatenate([lower * cosine + upper * sine, upper * cosine - lower * sine], axis=2)
    return turned.reshape(rows, -1).astype(jnp.bfloat16)


def adam_update(gradient, weights, first, second):
    first_new = beta_one * first + (1.0 - beta_one) * gradient
    second_new = beta_two * second + (1.0 - beta_two) * gradient * gradient
    ratio = first_new / bias_one / (jnp.sqrt(second_new / bias_two) + adam_eps)
    return weights - inner_rate * (ratio + decay_rate * weights)


def local_tiles(drift_rows, tile_rows, first_row):
    ends = jnp.cumsum(tile_rows, dtype=jnp.int32)
    starts = ends - tile_rows
    rows = first_row + jnp.arange(drift_rows.shape[0], dtype=jnp.int32)
    member = ((rows[:, None] >= starts[None, :]) & (rows[:, None] < ends[None, :])).astype(
        jnp.float32
    )
    return jnp.dot(jnp.sum(drift_rows, axis=1), member, precision=lax.Precision.HIGHEST)


def body(
    activations,
    key_cotangents,
    master,
    momentum,
    island_weights,
    first_moment,
    second_moment,
    tile_rows,
):
    own_rows = master.shape[0]
    tok_rows = key_cotangents.shape[1]
    chips = lax.axis_size("chip")
    core = lax.axis_index("core")
    position = lax.axis_index("chip") * 2 + core
    swap = [(0, 1), (1, 0)]
    unrotated = unrotate(key_cotangents[0], position * tok_rows)
    tokens = activations[0]

    def parity(side):
        return [
            lax.dynamic_slice_in_dim(tokens, (2 * k + side) * own_rows, own_rows, axis=1)
            for k in range(chips)
        ]

    their_tokens = [lax.ppermute(block, "core", swap) for block in parity(1 - core)]
    their_unrotated = lax.ppermute(unrotated, "core", swap)
    contract = (((0,), (0,)), ((), ()))
    partial = lax.dot_general(
        unrotated, jnp.stack(parity(core), axis=1), contract, preferred_element_type=jnp.float32
    ) + lax.dot_general(
        their_unrotated, jnp.stack(their_tokens, axis=1), contract,
        preferred_element_type=jnp.float32,
    )
    gradient = lax.psum_scatter(partial, "chip", scatter_dimension=1, tiled=True)
    gradient = with_layout_constraint(gradient, Layout((0, 1, 2)))
    gradient = with_layout_constraint(
        gradient.reshape(gradient.shape[0], own_rows).T, Layout((0, 1))
    )
    squares = lax.psum(jnp.sum(gradient * gradient), ("chip", "core"))
    factor = 1.0 / jnp.sqrt(squares + norm_epsilon)
    inner = adam_update(gradient * factor, island_weights[0], first_moment[0], second_moment[0])
    island_drift = master - inner
    replicas = lax.axis_size("island")
    drift = lax.psum(island_drift, "island") / replicas
    momentum_out = outer_moment * momentum + drift
    master_out = master - outer_rate * (drift + outer_moment * momentum_out)
    first_row = position * own_rows
    totals = (
        lax.psum(local_tiles(island_drift, tile_rows, first_row), ("island", "chip", "core"))
        / replicas
    )
    tile_sums = totals / jnp.sqrt(tile_rows.astype(jnp.float32) * master.shape[1])
    return (master_out, momentum_out, tile_sums)


def solution(mesh):
    islands, fsdp = mesh.devices.shape
    cores = jax.sharding.Mesh(
        mesh.devices.reshape(islands, fsdp // 2, 2), ("island", "chip", "core")
    )
    rows = ("chip", "core")
    placed = (
        P("island", rows, None),
        P("island", rows, None),
        P(rows, None),
        P(rows, None),
        P("island", rows, None),
        P("island", rows, None),
        P("island", rows, None),
        P(),
    )
    return jax.shard_map(
        body,
        mesh=cores,
        in_specs=placed,
        out_specs=(P(rows, None), P(rows, None), P()),
        check_vma=False,
    )
```

```python
import jax
import jax.numpy as jnp
from jax import lax
from jax.experimental.layout import Layout, with_layout_constraint
from jax.sharding import PartitionSpec as P

HEAD = 128
SEQ = 8192


beta_one = 0.9
beta_two = 0.95
bias_one = 1.0 - 0.9**3
bias_two = 1.0 - 0.95**3
inner_rate = 0.5
decay_rate = 0.1
outer_rate = 0.7
outer_moment = 0.9
adam_eps = 1e-08
norm_epsilon = 1e-06
rope_base = 500000.0


def unrotate(cotangent, first_row):
    rows = cotangent.shape[0]
    half = HEAD // 2
    positions = ((first_row + jnp.arange(rows, dtype=jnp.int32)) % SEQ).astype(jnp.float32)
    rates = rope_base ** (-2.0 * jnp.arange(half).astype(jnp.float32) / HEAD)
    angles = positions[:, None] * rates[None, :]
    cosine = jnp.cos(angles)[:, None, :]
    sine = jnp.sin(angles)[:, None, :]
    heads = cotangent.astype(jnp.float32).reshape(rows, -1, HEAD)
    lower = heads[:, :, :half]
    upper = heads[:, :, half:]
    turned = jnp.concatenate([lower * cosine + upper * sine, upper * cosine - lower * sine], axis=2)
    return turned.reshape(rows, -1).astype(jnp.bfloat16)


def adam_update(gradient, weights, first, second):
    first_new = beta_one * first + (1.0 - beta_one) * gradient
    second_new = beta_two * second + (1.0 - beta_two) * gradient * gradient
    ratio = first_new / bias_one / (jnp.sqrt(second_new / bias_two) + adam_eps)
    return weights - inner_rate * (ratio + decay_rate * weights)


def local_tiles(drift_rows, tile_rows, first_row):
    ends = jnp.cumsum(tile_rows, dtype=jnp.int32)
    starts = ends - tile_rows
    rows = first_row + jnp.arange(drift_rows.shape[0], dtype=jnp.int32)
    member = ((rows[:, None] >= starts[None, :]) & (rows[:, None] < ends[None, :])).astype(
        jnp.float32
    )
    return jnp.dot(jnp.sum(drift_rows, axis=1), member, precision=lax.Precision.HIGHEST)


def chip_scatter(partial, chips):
    core = lax.axis_index("core")
    chip = lax.axis_index("chip")
    along_x, along_y = chip % 2, chip // 2
    first = jnp.where(core == 0, along_x, along_y)
    second = jnp.where(core == 0, along_y, along_x)
    lanes = ("chip", "core")
    cross_first = [(f, f ^ 2) if f % 2 == 0 else (f, f ^ 4) for f in range(2 * chips)]
    cross_second = [(f, f ^ 4) if f % 2 == 0 else (f, f ^ 2) for f in range(2 * chips)]
    grid = partial.reshape(partial.shape[0], 2, 2, partial.shape[2])
    by_x = [grid[:, :, 0], grid[:, :, 1]]
    by_y = [grid[:, 0], grid[:, 1]]
    lower = jnp.where(core == 0, by_x[0], by_y[0])
    upper = jnp.where(core == 0, by_x[1], by_y[1])
    keep = jnp.where(first == 0, lower, upper)
    send = jnp.where(first == 0, upper, lower)
    held = keep + lax.ppermute(send, lanes, cross_first)
    keep = jnp.where(second == 0, held[:, 0], held[:, 1])
    send = jnp.where(second == 0, held[:, 1], held[:, 0])
    return (keep + lax.ppermute(send, lanes, cross_second))[:, None]


def body(
    activations,
    key_cotangents,
    master,
    momentum,
    island_weights,
    first_moment,
    second_moment,
    tile_rows,
):
    own_rows = master.shape[0]
    tok_rows = key_cotangents.shape[1]
    chips = lax.axis_size("chip")
    core = lax.axis_index("core")
    position = lax.axis_index("chip") * 2 + core
    swap = [(0, 1), (1, 0)]
    unrotated = unrotate(key_cotangents[0], position * tok_rows)
    tokens = activations[0]

    def parity(side):
        return [
            lax.dynamic_slice_in_dim(tokens, (2 * k + side) * own_rows, own_rows, axis=1)
            for k in range(chips)
        ]

    their_tokens = [lax.ppermute(block, "core", swap) for block in parity(1 - core)]
    their_unrotated = lax.ppermute(unrotated, "core", swap)
    contract = (((0,), (0,)), ((), ()))
    partial = lax.dot_general(
        unrotated, jnp.stack(parity(core), axis=1), contract, preferred_element_type=jnp.float32
    ) + lax.dot_general(
        their_unrotated, jnp.stack(their_tokens, axis=1), contract,
        preferred_element_type=jnp.float32,
    )
    if chips == 4:
        split = partial.shape[0] // 2
        gradient = jnp.concatenate(
            [
                lax.psum_scatter(partial[:split], "chip", scatter_dimension=1, tiled=True),
                chip_scatter(partial[split:], chips),
            ],
            axis=0,
        )
    else:
        gradient = lax.psum_scatter(partial, "chip", scatter_dimension=1, tiled=True)
    gradient = with_layout_constraint(gradient, Layout((0, 1, 2)))
    gradient = with_layout_constraint(
        gradient.reshape(gradient.shape[0], own_rows).T, Layout((0, 1))
    )
    squares = lax.psum(jnp.sum(gradient * gradient), ("chip", "core"))
    factor = 1.0 / jnp.sqrt(squares + norm_epsilon)
    inner = adam_update(gradient * factor, island_weights[0], first_moment[0], second_moment[0])
    island_drift = master - inner
    replicas = lax.axis_size("island")
    drift = lax.psum(island_drift, "island") / replicas
    momentum_out = outer_moment * momentum + drift
    master_out = master - outer_rate * (drift + outer_moment * momentum_out)
    first_row = position * own_rows
    totals = (
        lax.psum(local_tiles(island_drift, tile_rows, first_row), ("island", "chip", "core"))
        / replicas
    )
    tile_sums = totals / jnp.sqrt(tile_rows.astype(jnp.float32) * master.shape[1])
    return (master_out, momentum_out, tile_sums)


def solution(mesh):
    islands, fsdp = mesh.devices.shape
    cores = jax.sharding.Mesh(
        mesh.devices.reshape(islands, fsdp // 2, 2), ("island", "chip", "core")
    )
    rows = ("chip", "core")
    placed = (
        P("island", rows, None),
        P("island", rows, None),
        P(rows, None),
        P(rows, None),
        P("island", rows, None),
        P("island", rows, None),
        P("island", rows, None),
        P(),
    )
    return jax.shard_map(
        body,
        mesh=cores,
        in_specs=placed,
        out_specs=(P(rows, None), P(rows, None), P()),
        check_vma=False,
    )
```

```python
import jax
import jax.numpy as jnp
from jax import lax
from jax.experimental.layout import Layout, with_layout_constraint
from jax.sharding import PartitionSpec as P

HEAD = 128
SEQ = 8192


beta_one = 0.9
beta_two = 0.95
bias_one = 1.0 - 0.9**3
bias_two = 1.0 - 0.95**3
inner_rate = 0.5
decay_rate = 0.1
outer_rate = 0.7
outer_moment = 0.9
adam_eps = 1e-08
norm_epsilon = 1e-06
rope_base = 500000.0


def unrotate(cotangent, first_row):
    rows = cotangent.shape[0]
    half = HEAD // 2
    positions = ((first_row + jnp.arange(rows, dtype=jnp.int32)) % SEQ).astype(jnp.float32)
    rates = rope_base ** (-2.0 * jnp.arange(half).astype(jnp.float32) / HEAD)
    angles = positions[:, None] * rates[None, :]
    cosine = jnp.cos(angles)[:, None, :]
    sine = jnp.sin(angles)[:, None, :]
    heads = cotangent.astype(jnp.float32).reshape(rows, -1, HEAD)
    lower = heads[:, :, :half]
    upper = heads[:, :, half:]
    turned = jnp.concatenate([lower * cosine + upper * sine, upper * cosine - lower * sine], axis=2)
    return turned.reshape(rows, -1).astype(jnp.bfloat16)


def adam_update(gradient, weights, first, second):
    first_new = beta_one * first + (1.0 - beta_one) * gradient
    second_new = beta_two * second + (1.0 - beta_two) * gradient * gradient
    ratio = first_new / bias_one / (jnp.sqrt(second_new / bias_two) + adam_eps)
    return weights - inner_rate * (ratio + decay_rate * weights)


def local_tiles(drift_rows, tile_rows, first_row):
    ends = jnp.cumsum(tile_rows, dtype=jnp.int32)
    starts = ends - tile_rows
    rows = first_row + jnp.arange(drift_rows.shape[0], dtype=jnp.int32)
    member = ((rows[:, None] >= starts[None, :]) & (rows[:, None] < ends[None, :])).astype(
        jnp.float32
    )
    return jnp.dot(jnp.sum(drift_rows, axis=1), member, precision=lax.Precision.HIGHEST)


def chip_scatter(partial, chips):
    core = lax.axis_index("core")
    chip = lax.axis_index("chip")
    along_x, along_y = chip % 2, chip // 2
    first = jnp.where(core == 0, along_x, along_y)
    second = jnp.where(core == 0, along_y, along_x)
    lanes = ("chip", "core")
    cross_first = [(f, f ^ 2) if f % 2 == 0 else (f, f ^ 4) for f in range(2 * chips)]
    cross_second = [(f, f ^ 4) if f % 2 == 0 else (f, f ^ 2) for f in range(2 * chips)]
    grid = partial.reshape(partial.shape[0], 2, 2, partial.shape[2])
    by_x = [grid[:, :, 0], grid[:, :, 1]]
    by_y = [grid[:, 0], grid[:, 1]]
    lower = jnp.where(core == 0, by_x[0], by_y[0])
    upper = jnp.where(core == 0, by_x[1], by_y[1])
    keep = jnp.where(first == 0, lower, upper)
    send = jnp.where(first == 0, upper, lower)
    held = keep + lax.ppermute(send, lanes, cross_first)
    keep = jnp.where(second == 0, held[:, 0], held[:, 1])
    send = jnp.where(second == 0, held[:, 1], held[:, 0])
    return (keep + lax.ppermute(send, lanes, cross_second))[:, None]


def body(
    activations,
    key_cotangents,
    master,
    momentum,
    island_weights,
    first_moment,
    second_moment,
    tile_rows,
):
    own_rows = master.shape[0]
    tok_rows = key_cotangents.shape[1]
    chips = lax.axis_size("chip")
    core = lax.axis_index("core")
    position = lax.axis_index("chip") * 2 + core
    swap = [(0, 1), (1, 0)]
    unrotated = unrotate(key_cotangents[0], position * tok_rows)
    tokens = activations[0]

    def parity(side):
        return [
            lax.dynamic_slice_in_dim(tokens, (2 * k + side) * own_rows, own_rows, axis=1)
            for k in range(chips)
        ]

    their_tokens = [lax.ppermute(block, "core", swap) for block in parity(1 - core)]
    their_unrotated = lax.ppermute(unrotated, "core", swap)
    contract = (((0,), (0,)), ((), ()))
    partial = lax.dot_general(
        unrotated, jnp.stack(parity(core), axis=1), contract, preferred_element_type=jnp.float32
    ) + lax.dot_general(
        their_unrotated, jnp.stack(their_tokens, axis=1), contract,
        preferred_element_type=jnp.float32,
    )
    def rows_major(block):
        block = with_layout_constraint(block, Layout((0, 1, 2)))
        return with_layout_constraint(block.reshape(block.shape[0], own_rows).T, Layout((0, 1)))

    if chips == 4:
        split = partial.shape[0] // 2
        gradient = jnp.concatenate(
            [
                rows_major(
                    lax.psum_scatter(partial[:split], "chip", scatter_dimension=1, tiled=True)
                ),
                rows_major(chip_scatter(partial[split:], chips)),
            ],
            axis=1,
        )
    else:
        gradient = rows_major(lax.psum_scatter(partial, "chip", scatter_dimension=1, tiled=True))
    squares = lax.psum(jnp.sum(gradient * gradient), ("chip", "core"))
    factor = 1.0 / jnp.sqrt(squares + norm_epsilon)
    inner = adam_update(gradient * factor, island_weights[0], first_moment[0], second_moment[0])
    island_drift = master - inner
    replicas = lax.axis_size("island")
    drift = lax.psum(island_drift, "island") / replicas
    momentum_out = outer_moment * momentum + drift
    master_out = master - outer_rate * (drift + outer_moment * momentum_out)
    first_row = position * own_rows
    totals = (
        lax.psum(local_tiles(island_drift, tile_rows, first_row), ("island", "chip", "core"))
        / replicas
    )
    tile_sums = totals / jnp.sqrt(tile_rows.astype(jnp.float32) * master.shape[1])
    return (master_out, momentum_out, tile_sums)


def solution(mesh):
    islands, fsdp = mesh.devices.shape
    cores = jax.sharding.Mesh(
        mesh.devices.reshape(islands, fsdp // 2, 2), ("island", "chip", "core")
    )
    rows = ("chip", "core")
    placed = (
        P("island", rows, None),
        P("island", rows, None),
        P(rows, None),
        P(rows, None),
        P("island", rows, None),
        P("island", rows, None),
        P("island", rows, None),
        P(),
    )
    return jax.shard_map(
        body,
        mesh=cores,
        in_specs=placed,
        out_specs=(P(rows, None), P(rows, None), P()),
        check_vma=False,
    )
```

```python
import jax
import jax.numpy as jnp
from jax import lax
from jax.experimental.layout import Layout, with_layout_constraint
from jax.sharding import PartitionSpec as P

HEAD = 128
SEQ = 8192


beta_one = 0.9
beta_two = 0.95
bias_one = 1.0 - 0.9**3
bias_two = 1.0 - 0.95**3
inner_rate = 0.5
decay_rate = 0.1
outer_rate = 0.7
outer_moment = 0.9
adam_eps = 1e-08
norm_epsilon = 1e-06
rope_base = 500000.0


def unrotate(cotangent, first_row):
    rows = cotangent.shape[0]
    half = HEAD // 2
    positions = ((first_row + jnp.arange(rows, dtype=jnp.int32)) % SEQ).astype(jnp.float32)
    rates = rope_base ** (-2.0 * jnp.arange(half).astype(jnp.float32) / HEAD)
    angles = positions[:, None] * rates[None, :]
    cosine = jnp.cos(angles)[:, None, :]
    sine = jnp.sin(angles)[:, None, :]
    heads = cotangent.astype(jnp.float32).reshape(rows, -1, HEAD)
    lower = heads[:, :, :half]
    upper = heads[:, :, half:]
    turned = jnp.concatenate([lower * cosine + upper * sine, upper * cosine - lower * sine], axis=2)
    return turned.reshape(rows, -1).astype(jnp.bfloat16)


def adam_update(gradient, weights, first, second):
    first_new = beta_one * first + (1.0 - beta_one) * gradient
    second_new = beta_two * second + (1.0 - beta_two) * gradient * gradient
    ratio = first_new / bias_one / (jnp.sqrt(second_new / bias_two) + adam_eps)
    return weights - inner_rate * (ratio + decay_rate * weights)


def local_tiles(drift_rows, tile_rows, first_row):
    ends = jnp.cumsum(tile_rows, dtype=jnp.int32)
    starts = ends - tile_rows
    rows = first_row + jnp.arange(drift_rows.shape[0], dtype=jnp.int32)
    member = ((rows[:, None] >= starts[None, :]) & (rows[:, None] < ends[None, :])).astype(
        jnp.float32
    )
    return jnp.dot(jnp.sum(drift_rows, axis=1), member, precision=lax.Precision.HIGHEST)


def chip_scatter(partial, chips):
    core = lax.axis_index("core")
    chip = lax.axis_index("chip")
    along_x, along_y = chip % 2, chip // 2
    first = jnp.where(core == 0, along_x, along_y)
    second = jnp.where(core == 0, along_y, along_x)
    lanes = ("chip", "core")
    cross_first = [(f, f ^ 2) if f % 2 == 0 else (f, f ^ 4) for f in range(2 * chips)]
    cross_second = [(f, f ^ 4) if f % 2 == 0 else (f, f ^ 2) for f in range(2 * chips)]
    grid = partial.reshape(partial.shape[0], 2, 2, partial.shape[2])
    by_x = [grid[:, :, 0], grid[:, :, 1]]
    by_y = [grid[:, 0], grid[:, 1]]
    lower = jnp.where(core == 0, by_x[0], by_y[0])
    upper = jnp.where(core == 0, by_x[1], by_y[1])
    keep = jnp.where(first == 0, lower, upper)
    send = jnp.where(first == 0, upper, lower)
    held = keep + lax.ppermute(send, lanes, cross_first)
    keep = jnp.where(second == 0, held[:, 0], held[:, 1])
    send = jnp.where(second == 0, held[:, 1], held[:, 0])
    return (keep + lax.ppermute(send, lanes, cross_second))[:, None]


def island_tree(values):
    island = lax.axis_index("island")
    pair = values + lax.ppermute(values, "island", [(0, 1), (3, 2)])
    whole = pair + lax.ppermute(pair, "island", [(1, 2), (2, 1)])
    back = lax.ppermute(whole, "island", [(1, 0), (2, 3)])
    return jnp.where((island == 1) | (island == 2), whole, back)


def body(
    activations,
    key_cotangents,
    master,
    momentum,
    island_weights,
    first_moment,
    second_moment,
    tile_rows,
):
    own_rows = master.shape[0]
    tok_rows = key_cotangents.shape[1]
    chips = lax.axis_size("chip")
    core = lax.axis_index("core")
    position = lax.axis_index("chip") * 2 + core
    swap = [(0, 1), (1, 0)]
    unrotated = unrotate(key_cotangents[0], position * tok_rows)
    tokens = activations[0]

    def parity(side):
        return [
            lax.dynamic_slice_in_dim(tokens, (2 * k + side) * own_rows, own_rows, axis=1)
            for k in range(chips)
        ]

    their_tokens = [lax.ppermute(block, "core", swap) for block in parity(1 - core)]
    their_unrotated = lax.ppermute(unrotated, "core", swap)
    contract = (((0,), (0,)), ((), ()))
    partial = lax.dot_general(
        unrotated, jnp.stack(parity(core), axis=1), contract, preferred_element_type=jnp.float32
    ) + lax.dot_general(
        their_unrotated, jnp.stack(their_tokens, axis=1), contract,
        preferred_element_type=jnp.float32,
    )
    def rows_major(block):
        block = with_layout_constraint(block, Layout((0, 1, 2)))
        return with_layout_constraint(block.reshape(block.shape[0], own_rows).T, Layout((0, 1)))

    if chips == 4:
        split = partial.shape[0] // 2
        gradient = jnp.concatenate(
            [
                rows_major(
                    lax.psum_scatter(partial[:split], "chip", scatter_dimension=1, tiled=True)
                ),
                rows_major(chip_scatter(partial[split:], chips)),
            ],
            axis=1,
        )
    else:
        gradient = rows_major(lax.psum_scatter(partial, "chip", scatter_dimension=1, tiled=True))
    squares = lax.psum(jnp.sum(gradient * gradient), ("chip", "core"))
    factor = 1.0 / jnp.sqrt(squares + norm_epsilon)
    inner = adam_update(gradient * factor, island_weights[0], first_moment[0], second_moment[0])
    island_drift = master - inner
    replicas = lax.axis_size("island")
    if replicas == 4:
        split = own_rows * 5 // 8
        drift = jnp.concatenate(
            [lax.psum(island_drift[:split], "island"), island_tree(island_drift[split:])], axis=0
        ) / replicas
    else:
        drift = lax.psum(island_drift, "island") / replicas
    momentum_out = outer_moment * momentum + drift
    master_out = master - outer_rate * (drift + outer_moment * momentum_out)
    first_row = position * own_rows
    totals = (
        lax.psum(
            lax.psum(lax.psum(local_tiles(island_drift, tile_rows, first_row), "core"), "chip"),
            "island",
        )
        / replicas
    )
    tile_sums = totals / jnp.sqrt(tile_rows.astype(jnp.float32) * master.shape[1])
    return (master_out, momentum_out, tile_sums)


def solution(mesh):
    islands, fsdp = mesh.devices.shape
    cores = jax.sharding.Mesh(
        mesh.devices.reshape(islands, fsdp // 2, 2), ("island", "chip", "core")
    )
    rows = ("chip", "core")
    placed = (
        P("island", rows, None),
        P("island", rows, None),
        P(rows, None),
        P(rows, None),
        P("island", rows, None),
        P("island", rows, None),
        P("island", rows, None),
        P(),
    )
    return jax.shard_map(
        body,
        mesh=cores,
        in_specs=placed,
        out_specs=(P(rows, None), P(rows, None), P()),
        check_vma=False,
    )
```

```python
import jax
import jax.numpy as jnp
from jax import lax
from jax.experimental.layout import Layout, with_layout_constraint
from jax.sharding import PartitionSpec as P

HEAD = 128
SEQ = 8192


beta_one = 0.9
beta_two = 0.95
bias_one = 1.0 - 0.9**3
bias_two = 1.0 - 0.95**3
inner_rate = 0.5
decay_rate = 0.1
outer_rate = 0.7
outer_moment = 0.9
adam_eps = 1e-08
norm_epsilon = 1e-06
rope_base = 500000.0


def unrotate(cotangent, first_row):
    rows = cotangent.shape[0]
    half = HEAD // 2
    positions = ((first_row + jnp.arange(rows, dtype=jnp.int32)) % SEQ).astype(jnp.float32)
    rates = rope_base ** (-2.0 * jnp.arange(half).astype(jnp.float32) / HEAD)
    angles = positions[:, None] * rates[None, :]
    cosine = jnp.cos(angles)[:, None, :]
    sine = jnp.sin(angles)[:, None, :]
    heads = cotangent.astype(jnp.float32).reshape(rows, -1, HEAD)
    lower = heads[:, :, :half]
    upper = heads[:, :, half:]
    turned = jnp.concatenate([lower * cosine + upper * sine, upper * cosine - lower * sine], axis=2)
    return turned.reshape(rows, -1).astype(jnp.bfloat16)


def adam_update(gradient, weights, first, second):
    first_new = beta_one * first + (1.0 - beta_one) * gradient
    second_new = beta_two * second + (1.0 - beta_two) * gradient * gradient
    ratio = first_new / bias_one / (jnp.sqrt(second_new / bias_two) + adam_eps)
    return weights - inner_rate * (ratio + decay_rate * weights)


def local_tiles(drift_rows, tile_rows, first_row):
    ends = jnp.cumsum(tile_rows, dtype=jnp.int32)
    starts = ends - tile_rows
    rows = first_row + jnp.arange(drift_rows.shape[0], dtype=jnp.int32)
    member = ((rows[:, None] >= starts[None, :]) & (rows[:, None] < ends[None, :])).astype(
        jnp.float32
    )
    return jnp.dot(jnp.sum(drift_rows, axis=1), member, precision=lax.Precision.HIGHEST)


def chip_scatter(partial, chips):
    core = lax.axis_index("core")
    chip = lax.axis_index("chip")
    along_x, along_y = chip % 2, chip // 2
    first = jnp.where(core == 0, along_x, along_y)
    second = jnp.where(core == 0, along_y, along_x)
    lanes = ("chip", "core")
    cross_first = [(f, f ^ 2) if f % 2 == 0 else (f, f ^ 4) for f in range(2 * chips)]
    cross_second = [(f, f ^ 4) if f % 2 == 0 else (f, f ^ 2) for f in range(2 * chips)]
    grid = partial.reshape(partial.shape[0], 2, 2, partial.shape[2])
    by_x = [grid[:, :, 0], grid[:, :, 1]]
    by_y = [grid[:, 0], grid[:, 1]]
    lower = jnp.where(core == 0, by_x[0], by_y[0])
    upper = jnp.where(core == 0, by_x[1], by_y[1])
    keep = jnp.where(first == 0, lower, upper)
    send = jnp.where(first == 0, upper, lower)
    held = keep + lax.ppermute(send, lanes, cross_first)
    keep = jnp.where(second == 0, held[:, 0], held[:, 1])
    send = jnp.where(second == 0, held[:, 1], held[:, 0])
    return (keep + lax.ppermute(send, lanes, cross_second))[:, None]


def island_tree(values):
    island = lax.axis_index("island")
    pair = values + lax.ppermute(values, "island", [(0, 1), (3, 2)])
    whole = pair + lax.ppermute(pair, "island", [(1, 2), (2, 1)])
    back = lax.ppermute(whole, "island", [(1, 0), (2, 3)])
    return jnp.where((island == 1) | (island == 2), whole, back)


def body(
    activations,
    key_cotangents,
    master,
    momentum,
    island_weights,
    first_moment,
    second_moment,
    tile_rows,
):
    own_rows = master.shape[0]
    tok_rows = key_cotangents.shape[1]
    chips = lax.axis_size("chip")
    core = lax.axis_index("core")
    position = lax.axis_index("chip") * 2 + core
    swap = [(0, 1), (1, 0)]
    unrotated = unrotate(key_cotangents[0], position * tok_rows)
    tokens = activations[0]

    def parity(side):
        return [
            lax.dynamic_slice_in_dim(tokens, (2 * k + side) * own_rows, own_rows, axis=1)
            for k in range(chips)
        ]

    their_tokens = [lax.ppermute(block, "core", swap) for block in parity(1 - core)]
    their_unrotated = lax.ppermute(unrotated, "core", swap)
    contract = (((0,), (0,)), ((), ()))
    partial = lax.dot_general(
        unrotated, jnp.stack(parity(core), axis=1), contract, preferred_element_type=jnp.float32
    ) + lax.dot_general(
        their_unrotated, jnp.stack(their_tokens, axis=1), contract,
        preferred_element_type=jnp.float32,
    )
    def rows_major(block):
        block = with_layout_constraint(block, Layout((0, 1, 2)))
        return with_layout_constraint(block.reshape(block.shape[0], own_rows).T, Layout((0, 1)))

    if chips == 4:
        split = partial.shape[0] // 2
        gradient = jnp.concatenate(
            [
                rows_major(
                    lax.psum_scatter(partial[:split], "chip", scatter_dimension=1, tiled=True)
                ),
                rows_major(chip_scatter(partial[split:], chips)),
            ],
            axis=1,
        )
    else:
        gradient = rows_major(lax.psum_scatter(partial, "chip", scatter_dimension=1, tiled=True))
    squares = lax.psum(jnp.sum(gradient * gradient), ("chip", "core"))
    factor = 1.0 / jnp.sqrt(squares + norm_epsilon)
    inner = adam_update(gradient * factor, island_weights[0], first_moment[0], second_moment[0])
    island_drift = master - inner
    replicas = lax.axis_size("island")
    if replicas == 4:
        split = own_rows * 5 // 8
        drift = jnp.concatenate(
            [lax.psum(island_drift[:split], "island"), island_tree(island_drift[split:])], axis=0
        ) / replicas
    else:
        drift = lax.psum(island_drift, "island") / replicas
    momentum_out = outer_moment * momentum + drift
    master_out = master - outer_rate * (drift + outer_moment * momentum_out)
    first_row = position * own_rows
    totals = (
        lax.psum(local_tiles(drift, tile_rows, first_row), ("chip", "core"))
    )
    tile_sums = totals / jnp.sqrt(tile_rows.astype(jnp.float32) * master.shape[1])
    return (master_out, momentum_out, tile_sums)


def solution(mesh):
    islands, fsdp = mesh.devices.shape
    cores = jax.sharding.Mesh(
        mesh.devices.reshape(islands, fsdp // 2, 2), ("island", "chip", "core")
    )
    rows = ("chip", "core")
    placed = (
        P("island", rows, None),
        P("island", rows, None),
        P(rows, None),
        P(rows, None),
        P("island", rows, None),
        P("island", rows, None),
        P("island", rows, None),
        P(),
    )
    return jax.shard_map(
        body,
        mesh=cores,
        in_specs=placed,
        out_specs=(P(rows, None), P(rows, None), P()),
        check_vma=False,
    )
```

```python
import jax
import jax.numpy as jnp
from jax import lax
from jax.experimental.layout import Layout, with_layout_constraint
from jax.sharding import PartitionSpec as P

HEAD = 128
SEQ = 8192


beta_one = 0.9
beta_two = 0.95
bias_one = 1.0 - 0.9**3
bias_two = 1.0 - 0.95**3
inner_rate = 0.5
decay_rate = 0.1
outer_rate = 0.7
outer_moment = 0.9
adam_eps = 1e-08
norm_epsilon = 1e-06
rope_base = 500000.0


def unrotate(cotangent, first_row):
    rows = cotangent.shape[0]
    half = HEAD // 2
    positions = ((first_row + jnp.arange(rows, dtype=jnp.int32)) % SEQ).astype(jnp.float32)
    rates = rope_base ** (-2.0 * jnp.arange(half).astype(jnp.float32) / HEAD)
    angles = positions[:, None] * rates[None, :]
    cosine = jnp.cos(angles)[:, None, :]
    sine = jnp.sin(angles)[:, None, :]
    heads = cotangent.astype(jnp.float32).reshape(rows, -1, HEAD)
    lower = heads[:, :, :half]
    upper = heads[:, :, half:]
    turned = jnp.concatenate([lower * cosine + upper * sine, upper * cosine - lower * sine], axis=2)
    return turned.reshape(rows, -1).astype(jnp.bfloat16)


def adam_update(gradient, weights, first, second):
    first_new = beta_one * first + (1.0 - beta_one) * gradient
    second_new = beta_two * second + (1.0 - beta_two) * gradient * gradient
    ratio = first_new / bias_one / (jnp.sqrt(second_new / bias_two) + adam_eps)
    return weights - inner_rate * (ratio + decay_rate * weights)


def local_tiles(drift_rows, tile_rows, first_row):
    ends = jnp.cumsum(tile_rows, dtype=jnp.int32)
    starts = ends - tile_rows
    rows = first_row + jnp.arange(drift_rows.shape[0], dtype=jnp.int32)
    member = ((rows[:, None] >= starts[None, :]) & (rows[:, None] < ends[None, :])).astype(
        jnp.float32
    )
    return jnp.dot(jnp.sum(drift_rows, axis=1), member, precision=lax.Precision.HIGHEST)


def chip_scatter(partial, chips, tie):
    core = lax.axis_index("core")
    chip = lax.axis_index("chip")
    along_x, along_y = chip % 2, chip // 2
    first = jnp.where(core == 0, along_x, along_y)
    second = jnp.where(core == 0, along_y, along_x)
    lanes = ("chip", "core")
    cross_first = [(f, f ^ 2) if f % 2 == 0 else (f, f ^ 4) for f in range(2 * chips)]
    cross_second = [(f, f ^ 4) if f % 2 == 0 else (f, f ^ 2) for f in range(2 * chips)]
    grid = partial.reshape(partial.shape[0], 2, 2, partial.shape[2])
    by_x = [grid[:, :, 0], grid[:, :, 1]]
    by_y = [grid[:, 0], grid[:, 1]]
    lower = jnp.where(core == 0, by_x[0], by_y[0])
    upper = jnp.where(core == 0, by_x[1], by_y[1])
    keep = jnp.where(first == 0, lower, upper)
    send = jnp.where(first == 0, upper, lower)
    send, tie = lax.optimization_barrier((send, tie))
    held = keep + lax.ppermute(send, lanes, cross_first)
    keep = jnp.where(second == 0, held[:, 0], held[:, 1])
    send = jnp.where(second == 0, held[:, 1], held[:, 0])
    return (keep + lax.ppermute(send, lanes, cross_second))[:, None], tie


def body(
    activations,
    key_cotangents,
    master,
    momentum,
    island_weights,
    first_moment,
    second_moment,
    tile_rows,
):
    own_rows = master.shape[0]
    tok_rows = key_cotangents.shape[1]
    chips = lax.axis_size("chip")
    core = lax.axis_index("core")
    position = lax.axis_index("chip") * 2 + core
    swap = [(0, 1), (1, 0)]
    unrotated = unrotate(key_cotangents[0], position * tok_rows)
    tokens = activations[0]

    def parity(side):
        return [
            lax.dynamic_slice_in_dim(tokens, (2 * k + side) * own_rows, own_rows, axis=1)
            for k in range(chips)
        ]

    their_tokens = [lax.ppermute(block, "core", swap) for block in parity(1 - core)]
    their_unrotated = lax.ppermute(unrotated, "core", swap)
    contract = (((0,), (0,)), ((), ()))
    mine = jnp.stack(parity(core), axis=1)
    theirs = jnp.stack(their_tokens, axis=1)

    def product(own_lhs, their_lhs):
        return lax.dot_general(
            own_lhs, mine, contract, preferred_element_type=jnp.float32
        ) + lax.dot_general(their_lhs, theirs, contract, preferred_element_type=jnp.float32)

    def rows_major(block):
        block = with_layout_constraint(block, Layout((0, 1, 2)))
        return with_layout_constraint(block.reshape(block.shape[0], own_rows).T, Layout((0, 1)))

    if chips == 4:
        split = unrotated.shape[1] // 2
        sent, (own_lhs, their_lhs) = chip_scatter(
            product(unrotated[:, split:], their_unrotated[:, split:]),
            chips,
            (unrotated, their_unrotated),
        )
        summed = lax.psum_scatter(
            product(own_lhs[:, :split], their_lhs[:, :split]), "chip", scatter_dimension=1, tiled=True
        )
        gradient = jnp.concatenate([rows_major(summed), rows_major(sent)], axis=1)
    else:
        gradient = rows_major(
            lax.psum_scatter(
                product(unrotated, their_unrotated), "chip", scatter_dimension=1, tiled=True
            )
        )
    squares = lax.psum(jnp.sum(gradient * gradient), ("chip", "core"))
    factor = 1.0 / jnp.sqrt(squares + norm_epsilon)
    inner = adam_update(gradient * factor, island_weights[0], first_moment[0], second_moment[0])
    island_drift = master - inner
    replicas = lax.axis_size("island")
    drift = lax.psum(island_drift, "island") / replicas
    momentum_out = outer_moment * momentum + drift
    master_out = master - outer_rate * (drift + outer_moment * momentum_out)
    first_row = position * own_rows
    totals = (
        lax.psum(local_tiles(island_drift, tile_rows, first_row), ("island", "chip", "core"))
        / replicas
    )
    tile_sums = totals / jnp.sqrt(tile_rows.astype(jnp.float32) * master.shape[1])
    return (master_out, momentum_out, tile_sums)


def solution(mesh):
    islands, fsdp = mesh.devices.shape
    cores = jax.sharding.Mesh(
        mesh.devices.reshape(islands, fsdp // 2, 2), ("island", "chip", "core")
    )
    rows = ("chip", "core")
    placed = (
        P("island", rows, None),
        P("island", rows, None),
        P(rows, None),
        P(rows, None),
        P("island", rows, None),
        P("island", rows, None),
        P("island", rows, None),
        P(),
    )
    return jax.shard_map(
        body,
        mesh=cores,
        in_specs=placed,
        out_specs=(P(rows, None), P(rows, None), P()),
        check_vma=False,
    )
```

```python
import jax
import jax.numpy as jnp
from jax import lax
from jax.experimental.layout import Layout, with_layout_constraint
from jax.sharding import PartitionSpec as P

HEAD = 128
SEQ = 8192


beta_one = 0.9
beta_two = 0.95
bias_one = 1.0 - 0.9**3
bias_two = 1.0 - 0.95**3
inner_rate = 0.5
decay_rate = 0.1
outer_rate = 0.7
outer_moment = 0.9
adam_eps = 1e-08
norm_epsilon = 1e-06
rope_base = 500000.0


def unrotate(cotangent, first_row):
    rows = cotangent.shape[0]
    half = HEAD // 2
    positions = ((first_row + jnp.arange(rows, dtype=jnp.int32)) % SEQ).astype(jnp.float32)
    rates = rope_base ** (-2.0 * jnp.arange(half).astype(jnp.float32) / HEAD)
    angles = positions[:, None] * rates[None, :]
    cosine = jnp.cos(angles)[:, None, :]
    sine = jnp.sin(angles)[:, None, :]
    heads = cotangent.astype(jnp.float32).reshape(rows, -1, HEAD)
    lower = heads[:, :, :half]
    upper = heads[:, :, half:]
    turned = jnp.concatenate([lower * cosine + upper * sine, upper * cosine - lower * sine], axis=2)
    return turned.reshape(rows, -1).astype(jnp.bfloat16)


def adam_update(gradient, weights, first, second):
    first_new = beta_one * first + (1.0 - beta_one) * gradient
    second_new = beta_two * second + (1.0 - beta_two) * gradient * gradient
    ratio = first_new / bias_one / (jnp.sqrt(second_new / bias_two) + adam_eps)
    return weights - inner_rate * (ratio + decay_rate * weights)


def local_tiles(drift_rows, tile_rows, first_row):
    ends = jnp.cumsum(tile_rows, dtype=jnp.int32)
    starts = ends - tile_rows
    rows = first_row + jnp.arange(drift_rows.shape[0], dtype=jnp.int32)
    member = ((rows[:, None] >= starts[None, :]) & (rows[:, None] < ends[None, :])).astype(
        jnp.float32
    )
    return jnp.dot(jnp.sum(drift_rows, axis=1), member, precision=lax.Precision.HIGHEST)


def chip_scatter(partial, chips):
    core = lax.axis_index("core")
    chip = lax.axis_index("chip")
    along_x, along_y = chip % 2, chip // 2
    first = jnp.where(core == 0, along_x, along_y)
    second = jnp.where(core == 0, along_y, along_x)
    lanes = ("chip", "core")
    cross_first = [(f, f ^ 2) if f % 2 == 0 else (f, f ^ 4) for f in range(2 * chips)]
    cross_second = [(f, f ^ 4) if f % 2 == 0 else (f, f ^ 2) for f in range(2 * chips)]
    grid = partial.reshape(partial.shape[0], 2, 2, partial.shape[2])
    by_x = [grid[:, :, 0], grid[:, :, 1]]
    by_y = [grid[:, 0], grid[:, 1]]
    lower = jnp.where(core == 0, by_x[0], by_y[0])
    upper = jnp.where(core == 0, by_x[1], by_y[1])
    keep = jnp.where(first == 0, lower, upper)
    send = jnp.where(first == 0, upper, lower)
    held = keep + lax.ppermute(send, lanes, cross_first)
    keep = jnp.where(second == 0, held[:, 0], held[:, 1])
    send = jnp.where(second == 0, held[:, 1], held[:, 0])
    return (keep + lax.ppermute(send, lanes, cross_second))[:, None]


def body(
    activations,
    key_cotangents,
    master,
    momentum,
    island_weights,
    first_moment,
    second_moment,
    tile_rows,
):
    own_rows = master.shape[0]
    tok_rows = key_cotangents.shape[1]
    chips = lax.axis_size("chip")
    core = lax.axis_index("core")
    position = lax.axis_index("chip") * 2 + core
    swap = [(0, 1), (1, 0)]
    unrotated = unrotate(key_cotangents[0], position * tok_rows)
    tokens = activations[0]

    def parity(side):
        return [
            lax.dynamic_slice_in_dim(tokens, (2 * k + side) * own_rows, own_rows, axis=1)
            for k in range(chips)
        ]

    their_tokens = [lax.ppermute(block, "core", swap) for block in parity(1 - core)]
    their_unrotated = lax.ppermute(unrotated, "core", swap)
    contract = (((0,), (0,)), ((), ()))
    partial = lax.dot_general(
        unrotated, jnp.stack(parity(core), axis=1), contract, preferred_element_type=jnp.float32
    ) + lax.dot_general(
        their_unrotated, jnp.stack(their_tokens, axis=1), contract,
        preferred_element_type=jnp.float32,
    )
    def rows_major(block):
        block = with_layout_constraint(block, Layout((0, 1, 2)))
        return with_layout_constraint(block.reshape(block.shape[0], own_rows).T, Layout((0, 1)))

    if chips == 4:
        split = partial.shape[0] * 5 // 8
        gradient = jnp.concatenate(
            [
                rows_major(
                    lax.psum_scatter(partial[:split], "chip", scatter_dimension=1, tiled=True)
                ),
                rows_major(chip_scatter(partial[split:], chips)),
            ],
            axis=1,
        )
    else:
        gradient = rows_major(lax.psum_scatter(partial, "chip", scatter_dimension=1, tiled=True))
    squares = lax.psum(jnp.sum(gradient * gradient), ("chip", "core"))
    factor = 1.0 / jnp.sqrt(squares + norm_epsilon)
    inner = adam_update(gradient * factor, island_weights[0], first_moment[0], second_moment[0])
    island_drift = master - inner
    replicas = lax.axis_size("island")
    drift = lax.psum(island_drift, "island") / replicas
    momentum_out = outer_moment * momentum + drift
    master_out = master - outer_rate * (drift + outer_moment * momentum_out)
    first_row = position * own_rows
    totals = (
        lax.psum(local_tiles(island_drift, tile_rows, first_row), ("island", "chip", "core"))
        / replicas
    )
    tile_sums = totals / jnp.sqrt(tile_rows.astype(jnp.float32) * master.shape[1])
    return (master_out, momentum_out, tile_sums)


def solution(mesh):
    islands, fsdp = mesh.devices.shape
    cores = jax.sharding.Mesh(
        mesh.devices.reshape(islands, fsdp // 2, 2), ("island", "chip", "core")
    )
    rows = ("chip", "core")
    placed = (
        P("island", rows, None),
        P("island", rows, None),
        P(rows, None),
        P(rows, None),
        P("island", rows, None),
        P("island", rows, None),
        P("island", rows, None),
        P(),
    )
    return jax.shard_map(
        body,
        mesh=cores,
        in_specs=placed,
        out_specs=(P(rows, None), P(rows, None), P()),
        check_vma=False,
    )
```

```python
import jax
import jax.numpy as jnp
from jax import lax
from jax.experimental.layout import Layout, with_layout_constraint
from jax.sharding import PartitionSpec as P

HEAD = 128
SEQ = 8192


beta_one = 0.9
beta_two = 0.95
bias_one = 1.0 - 0.9**3
bias_two = 1.0 - 0.95**3
inner_rate = 0.5
decay_rate = 0.1
outer_rate = 0.7
outer_moment = 0.9
adam_eps = 1e-08
norm_epsilon = 1e-06
rope_base = 500000.0


def unrotate(cotangent, first_row):
    rows = cotangent.shape[0]
    half = HEAD // 2
    positions = ((first_row + jnp.arange(rows, dtype=jnp.int32)) % SEQ).astype(jnp.float32)
    rates = rope_base ** (-2.0 * jnp.arange(half).astype(jnp.float32) / HEAD)
    angles = positions[:, None] * rates[None, :]
    cosine = jnp.cos(angles)[:, None, :]
    sine = jnp.sin(angles)[:, None, :]
    heads = cotangent.astype(jnp.float32).reshape(rows, -1, HEAD)
    lower = heads[:, :, :half]
    upper = heads[:, :, half:]
    turned = jnp.concatenate([lower * cosine + upper * sine, upper * cosine - lower * sine], axis=2)
    return turned.reshape(rows, -1).astype(jnp.bfloat16)


def adam_update(gradient, weights, first, second):
    first_new = beta_one * first + (1.0 - beta_one) * gradient
    second_new = beta_two * second + (1.0 - beta_two) * gradient * gradient
    ratio = first_new / bias_one / (jnp.sqrt(second_new / bias_two) + adam_eps)
    return weights - inner_rate * (ratio + decay_rate * weights)


def local_tiles(drift_rows, tile_rows, first_row):
    ends = jnp.cumsum(tile_rows, dtype=jnp.int32)
    starts = ends - tile_rows
    rows = first_row + jnp.arange(drift_rows.shape[0], dtype=jnp.int32)
    member = ((rows[:, None] >= starts[None, :]) & (rows[:, None] < ends[None, :])).astype(
        jnp.float32
    )
    return jnp.dot(jnp.sum(drift_rows, axis=1), member, precision=lax.Precision.HIGHEST)


def chip_scatter(partial, chips):
    core = lax.axis_index("core")
    chip = lax.axis_index("chip")
    along_x, along_y = chip % 2, chip // 2
    first = jnp.where(core == 0, along_x, along_y)
    second = jnp.where(core == 0, along_y, along_x)
    lanes = ("chip", "core")
    cross_first = [(f, f ^ 2) if f % 2 == 0 else (f, f ^ 4) for f in range(2 * chips)]
    cross_second = [(f, f ^ 4) if f % 2 == 0 else (f, f ^ 2) for f in range(2 * chips)]
    grid = partial.reshape(partial.shape[0], 2, 2, partial.shape[2])
    by_x = [grid[:, :, 0], grid[:, :, 1]]
    by_y = [grid[:, 0], grid[:, 1]]
    lower = jnp.where(core == 0, by_x[0], by_y[0])
    upper = jnp.where(core == 0, by_x[1], by_y[1])
    keep = jnp.where(first == 0, lower, upper)
    send = jnp.where(first == 0, upper, lower)
    held = keep + lax.ppermute(send, lanes, cross_first)
    keep = jnp.where(second == 0, held[:, 0], held[:, 1])
    send = jnp.where(second == 0, held[:, 1], held[:, 0])
    return (keep + lax.ppermute(send, lanes, cross_second))[:, None]


def body(
    activations,
    key_cotangents,
    master,
    momentum,
    island_weights,
    first_moment,
    second_moment,
    tile_rows,
):
    own_rows = master.shape[0]
    tok_rows = key_cotangents.shape[1]
    chips = lax.axis_size("chip")
    core = lax.axis_index("core")
    position = lax.axis_index("chip") * 2 + core
    swap = [(0, 1), (1, 0)]
    unrotated = unrotate(key_cotangents[0], position * tok_rows)
    tokens = activations[0]

    def parity(side):
        return [
            lax.dynamic_slice_in_dim(tokens, (2 * k + side) * own_rows, own_rows, axis=1)
            for k in range(chips)
        ]

    their_tokens = [lax.ppermute(block, "core", swap) for block in parity(1 - core)]
    their_unrotated = lax.ppermute(unrotated, "core", swap)
    contract = (((0,), (0,)), ((), ()))
    partial = lax.dot_general(
        unrotated, jnp.stack(parity(core), axis=1), contract, preferred_element_type=jnp.float32
    ) + lax.dot_general(
        their_unrotated, jnp.stack(their_tokens, axis=1), contract,
        preferred_element_type=jnp.float32,
    )
    def rows_major(block):
        block = with_layout_constraint(block, Layout((0, 1, 2)))
        return with_layout_constraint(block.reshape(block.shape[0], own_rows).T, Layout((0, 1)))

    if chips == 4:
        split = partial.shape[0] * 3 // 8
        gradient = jnp.concatenate(
            [
                rows_major(
                    lax.psum_scatter(partial[:split], "chip", scatter_dimension=1, tiled=True)
                ),
                rows_major(chip_scatter(partial[split:], chips)),
            ],
            axis=1,
        )
    else:
        gradient = rows_major(lax.psum_scatter(partial, "chip", scatter_dimension=1, tiled=True))
    squares = lax.psum(jnp.sum(gradient * gradient), ("chip", "core"))
    factor = 1.0 / jnp.sqrt(squares + norm_epsilon)
    inner = adam_update(gradient * factor, island_weights[0], first_moment[0], second_moment[0])
    island_drift = master - inner
    replicas = lax.axis_size("island")
    drift = lax.psum(island_drift, "island") / replicas
    momentum_out = outer_moment * momentum + drift
    master_out = master - outer_rate * (drift + outer_moment * momentum_out)
    first_row = position * own_rows
    totals = (
        lax.psum(local_tiles(island_drift, tile_rows, first_row), ("island", "chip", "core"))
        / replicas
    )
    tile_sums = totals / jnp.sqrt(tile_rows.astype(jnp.float32) * master.shape[1])
    return (master_out, momentum_out, tile_sums)


def solution(mesh):
    islands, fsdp = mesh.devices.shape
    cores = jax.sharding.Mesh(
        mesh.devices.reshape(islands, fsdp // 2, 2), ("island", "chip", "core")
    )
    rows = ("chip", "core")
    placed = (
        P("island", rows, None),
        P("island", rows, None),
        P(rows, None),
        P(rows, None),
        P("island", rows, None),
        P("island", rows, None),
        P("island", rows, None),
        P(),
    )
    return jax.shard_map(
        body,
        mesh=cores,
        in_specs=placed,
        out_specs=(P(rows, None), P(rows, None), P()),
        check_vma=False,
    )
```

```python
import jax
import jax.numpy as jnp
from jax import lax
from jax.experimental.layout import Layout, with_layout_constraint
from jax.sharding import PartitionSpec as P

HEAD = 128
SEQ = 8192


beta_one = 0.9
beta_two = 0.95
bias_one = 1.0 - 0.9**3
bias_two = 1.0 - 0.95**3
inner_rate = 0.5
decay_rate = 0.1
outer_rate = 0.7
outer_moment = 0.9
adam_eps = 1e-08
norm_epsilon = 1e-06
rope_base = 500000.0


def unrotate(cotangent, first_row):
    rows = cotangent.shape[0]
    half = HEAD // 2
    positions = ((first_row + jnp.arange(rows, dtype=jnp.int32)) % SEQ).astype(jnp.float32)
    rates = rope_base ** (-2.0 * jnp.arange(half).astype(jnp.float32) / HEAD)
    angles = positions[:, None] * rates[None, :]
    cosine = jnp.cos(angles)[:, None, :]
    sine = jnp.sin(angles)[:, None, :]
    heads = cotangent.astype(jnp.float32).reshape(rows, -1, HEAD)
    lower = heads[:, :, :half]
    upper = heads[:, :, half:]
    turned = jnp.concatenate([lower * cosine + upper * sine, upper * cosine - lower * sine], axis=2)
    return turned.reshape(rows, -1).astype(jnp.bfloat16)


def adam_update(gradient, weights, first, second):
    first_new = beta_one * first + (1.0 - beta_one) * gradient
    second_new = beta_two * second + (1.0 - beta_two) * gradient * gradient
    ratio = first_new / bias_one / (jnp.sqrt(second_new / bias_two) + adam_eps)
    return weights - inner_rate * (ratio + decay_rate * weights)


def local_tiles(drift_rows, tile_rows, first_row):
    ends = jnp.cumsum(tile_rows, dtype=jnp.int32)
    starts = ends - tile_rows
    rows = first_row + jnp.arange(drift_rows.shape[0], dtype=jnp.int32)
    member = ((rows[:, None] >= starts[None, :]) & (rows[:, None] < ends[None, :])).astype(
        jnp.float32
    )
    return jnp.dot(jnp.sum(drift_rows, axis=1), member, precision=lax.Precision.HIGHEST)


def chip_scatter(partial, chips, after=None):
    core = lax.axis_index("core")
    chip = lax.axis_index("chip")
    along_x, along_y = chip % 2, chip // 2
    first = jnp.where(core == 0, along_x, along_y)
    second = jnp.where(core == 0, along_y, along_x)
    lanes = ("chip", "core")
    cross_first = [(f, f ^ 2) if f % 2 == 0 else (f, f ^ 4) for f in range(2 * chips)]
    cross_second = [(f, f ^ 4) if f % 2 == 0 else (f, f ^ 2) for f in range(2 * chips)]
    grid = partial.reshape(partial.shape[0], 2, 2, partial.shape[2])
    by_x = [grid[:, :, 0], grid[:, :, 1]]
    by_y = [grid[:, 0], grid[:, 1]]
    lower = jnp.where(core == 0, by_x[0], by_y[0])
    upper = jnp.where(core == 0, by_x[1], by_y[1])
    keep = jnp.where(first == 0, lower, upper)
    send = jnp.where(first == 0, upper, lower)
    if after is not None:
        send, _ = lax.optimization_barrier((send, after))
    arrived = lax.ppermute(send, lanes, cross_first)
    held = keep + arrived
    keep = jnp.where(second == 0, held[:, 0], held[:, 1])
    send = jnp.where(second == 0, held[:, 1], held[:, 0])
    return (keep + lax.ppermute(send, lanes, cross_second))[:, None], arrived


def body(
    activations,
    key_cotangents,
    master,
    momentum,
    island_weights,
    first_moment,
    second_moment,
    tile_rows,
):
    own_rows = master.shape[0]
    tok_rows = key_cotangents.shape[1]
    chips = lax.axis_size("chip")
    core = lax.axis_index("core")
    position = lax.axis_index("chip") * 2 + core
    swap = [(0, 1), (1, 0)]
    unrotated = unrotate(key_cotangents[0], position * tok_rows)
    tokens = activations[0]

    def parity(side):
        return [
            lax.dynamic_slice_in_dim(tokens, (2 * k + side) * own_rows, own_rows, axis=1)
            for k in range(chips)
        ]

    their_tokens = [lax.ppermute(block, "core", swap) for block in parity(1 - core)]
    their_unrotated = lax.ppermute(unrotated, "core", swap)
    contract = (((0,), (0,)), ((), ()))
    partial = lax.dot_general(
        unrotated, jnp.stack(parity(core), axis=1), contract, preferred_element_type=jnp.float32
    ) + lax.dot_general(
        their_unrotated, jnp.stack(their_tokens, axis=1), contract,
        preferred_element_type=jnp.float32,
    )
    def rows_major(block):
        block = with_layout_constraint(block, Layout((0, 1, 2)))
        return with_layout_constraint(block.reshape(block.shape[0], own_rows).T, Layout((0, 1)))

    def pieces(block):
        cut = block.shape[0] // 2
        first, arrived = chip_scatter(block[:cut], chips)
        second, _ = chip_scatter(block[cut:], chips, after=arrived)
        return rows_major(first), rows_major(second)

    if chips == 4:
        split = partial.shape[0] // 2
        gradient = jnp.concatenate(
            [
                rows_major(
                    lax.psum_scatter(partial[:split], "chip", scatter_dimension=1, tiled=True)
                ),
                *pieces(partial[split:]),
            ],
            axis=1,
        )
    else:
        gradient = rows_major(lax.psum_scatter(partial, "chip", scatter_dimension=1, tiled=True))
    squares = lax.psum(jnp.sum(gradient * gradient), ("chip", "core"))
    factor = 1.0 / jnp.sqrt(squares + norm_epsilon)
    inner = adam_update(gradient * factor, island_weights[0], first_moment[0], second_moment[0])
    island_drift = master - inner
    replicas = lax.axis_size("island")
    drift = lax.psum(island_drift, "island") / replicas
    momentum_out = outer_moment * momentum + drift
    master_out = master - outer_rate * (drift + outer_moment * momentum_out)
    first_row = position * own_rows
    totals = (
        lax.psum(local_tiles(island_drift, tile_rows, first_row), ("island", "chip", "core"))
        / replicas
    )
    tile_sums = totals / jnp.sqrt(tile_rows.astype(jnp.float32) * master.shape[1])
    return (master_out, momentum_out, tile_sums)


def solution(mesh):
    islands, fsdp = mesh.devices.shape
    cores = jax.sharding.Mesh(
        mesh.devices.reshape(islands, fsdp // 2, 2), ("island", "chip", "core")
    )
    rows = ("chip", "core")
    placed = (
        P("island", rows, None),
        P("island", rows, None),
        P(rows, None),
        P(rows, None),
        P("island", rows, None),
        P("island", rows, None),
        P("island", rows, None),
        P(),
    )
    return jax.shard_map(
        body,
        mesh=cores,
        in_specs=placed,
        out_specs=(P(rows, None), P(rows, None), P()),
        check_vma=False,
    )
```

```python
import jax
import jax.numpy as jnp
from jax import lax
from jax.experimental.layout import Layout, with_layout_constraint
from jax.sharding import PartitionSpec as P

HEAD = 128
SEQ = 8192


beta_one = 0.9
beta_two = 0.95
bias_one = 1.0 - 0.9**3
bias_two = 1.0 - 0.95**3
inner_rate = 0.5
decay_rate = 0.1
outer_rate = 0.7
outer_moment = 0.9
adam_eps = 1e-08
norm_epsilon = 1e-06
rope_base = 500000.0


def unrotate(cotangent, first_row):
    rows = cotangent.shape[0]
    half = HEAD // 2
    positions = ((first_row + jnp.arange(rows, dtype=jnp.int32)) % SEQ).astype(jnp.float32)
    rates = rope_base ** (-2.0 * jnp.arange(half).astype(jnp.float32) / HEAD)
    angles = positions[:, None] * rates[None, :]
    cosine = jnp.cos(angles)[:, None, :]
    sine = jnp.sin(angles)[:, None, :]
    heads = cotangent.astype(jnp.float32).reshape(rows, -1, HEAD)
    lower = heads[:, :, :half]
    upper = heads[:, :, half:]
    turned = jnp.concatenate([lower * cosine + upper * sine, upper * cosine - lower * sine], axis=2)
    return turned.reshape(rows, -1).astype(jnp.bfloat16)


def adam_update(gradient, weights, first, second):
    first_new = beta_one * first + (1.0 - beta_one) * gradient
    second_new = beta_two * second + (1.0 - beta_two) * gradient * gradient
    ratio = first_new / bias_one / (jnp.sqrt(second_new / bias_two) + adam_eps)
    return weights - inner_rate * (ratio + decay_rate * weights)


def local_tiles(drift_rows, tile_rows, first_row):
    ends = jnp.cumsum(tile_rows, dtype=jnp.int32)
    starts = ends - tile_rows
    rows = first_row + jnp.arange(drift_rows.shape[0], dtype=jnp.int32)
    member = ((rows[:, None] >= starts[None, :]) & (rows[:, None] < ends[None, :])).astype(
        jnp.float32
    )
    return jnp.dot(jnp.sum(drift_rows, axis=1), member, precision=lax.Precision.HIGHEST)


def chip_scatter(partial, chips):
    core = lax.axis_index("core")
    chip = lax.axis_index("chip")
    along_x, along_y = chip % 2, chip // 2
    first = jnp.where(core == 0, along_x, along_y)
    second = jnp.where(core == 0, along_y, along_x)
    lanes = ("chip", "core")
    cross_first = [(f, f ^ 2) if f % 2 == 0 else (f, f ^ 4) for f in range(2 * chips)]
    cross_second = [(f, f ^ 4) if f % 2 == 0 else (f, f ^ 2) for f in range(2 * chips)]
    grid = partial.reshape(partial.shape[0], 2, 2, partial.shape[2])
    by_x = [grid[:, :, 0], grid[:, :, 1]]
    by_y = [grid[:, 0], grid[:, 1]]
    lower = jnp.where(core == 0, by_x[0], by_y[0])
    upper = jnp.where(core == 0, by_x[1], by_y[1])
    keep = jnp.where(first == 0, lower, upper)
    send = jnp.where(first == 0, upper, lower)
    held = keep + lax.ppermute(send, lanes, cross_first)
    keep = jnp.where(second == 0, held[:, 0], held[:, 1])
    send = jnp.where(second == 0, held[:, 1], held[:, 0])
    return (keep + lax.ppermute(send, lanes, cross_second))[:, None]


def body(
    activations,
    key_cotangents,
    master,
    momentum,
    island_weights,
    first_moment,
    second_moment,
    tile_rows,
):
    own_rows = master.shape[0]
    tok_rows = key_cotangents.shape[1]
    chips = lax.axis_size("chip")
    core = lax.axis_index("core")
    position = lax.axis_index("chip") * 2 + core
    swap = [(0, 1), (1, 0)]
    unrotated = unrotate(key_cotangents[0], position * tok_rows)
    tokens = activations[0]

    def parity(side):
        return [
            lax.dynamic_slice_in_dim(tokens, (2 * k + side) * own_rows, own_rows, axis=1)
            for k in range(chips)
        ]

    their_tokens = [lax.ppermute(block, "core", swap) for block in parity(1 - core)]
    their_unrotated = lax.ppermute(unrotated, "core", swap)
    contract = (((0,), (0,)), ((), ()))
    partial = lax.dot_general(
        unrotated, jnp.stack(parity(core), axis=1), contract, preferred_element_type=jnp.float32
    ) + lax.dot_general(
        their_unrotated, jnp.stack(their_tokens, axis=1), contract,
        preferred_element_type=jnp.float32,
    )
    def rows_major(block):
        block = with_layout_constraint(block, Layout((0, 1, 2)))
        return with_layout_constraint(block.reshape(block.shape[0], own_rows).T, Layout((0, 1)))

    if chips == 4:
        split = partial.shape[0] * 9 // 16
        gradient = jnp.concatenate(
            [
                rows_major(
                    lax.psum_scatter(partial[:split], "chip", scatter_dimension=1, tiled=True)
                ),
                rows_major(chip_scatter(partial[split:], chips)),
            ],
            axis=1,
        )
    else:
        gradient = rows_major(lax.psum_scatter(partial, "chip", scatter_dimension=1, tiled=True))
    squares = lax.psum(jnp.sum(gradient * gradient), ("chip", "core"))
    factor = 1.0 / jnp.sqrt(squares + norm_epsilon)
    inner = adam_update(gradient * factor, island_weights[0], first_moment[0], second_moment[0])
    island_drift = master - inner
    replicas = lax.axis_size("island")
    drift = lax.psum(island_drift, "island") / replicas
    momentum_out = outer_moment * momentum + drift
    master_out = master - outer_rate * (drift + outer_moment * momentum_out)
    first_row = position * own_rows
    totals = (
        lax.psum(local_tiles(island_drift, tile_rows, first_row), ("island", "chip", "core"))
        / replicas
    )
    tile_sums = totals / jnp.sqrt(tile_rows.astype(jnp.float32) * master.shape[1])
    return (master_out, momentum_out, tile_sums)


def solution(mesh):
    islands, fsdp = mesh.devices.shape
    cores = jax.sharding.Mesh(
        mesh.devices.reshape(islands, fsdp // 2, 2), ("island", "chip", "core")
    )
    rows = ("chip", "core")
    placed = (
        P("island", rows, None),
        P("island", rows, None),
        P(rows, None),
        P(rows, None),
        P("island", rows, None),
        P("island", rows, None),
        P("island", rows, None),
        P(),
    )
    return jax.shard_map(
        body,
        mesh=cores,
        in_specs=placed,
        out_specs=(P(rows, None), P(rows, None), P()),
        check_vma=False,
    )
```
